512 devices in a mesh: seq: 64 (over z, y), tensor: 8 (over x, core).
Axes of the slice: x: 4, y: 4, z: 16, core: 2. Of those that a mesh axis runs over, the one named last changes fastest.
Arguments:
- hidden: bfloat16 [8192, 4096], P('seq', 'tensor')
- norm_gain: bfloat16 [4096], replicated, may hold values from 0.5 to 1.5
- w_query: bfloat16 [4096, 4096], P('seq', 'tensor')
- key_value_weight: bfloat16 [4096, 1024], P('seq')
- w_out: bfloat16 [4096, 4096], P('tensor', 'seq'), may hold values from -0.09375 to 0.09375
- prefix_key_cache: bfloat16 [64, 1024, 1024], P('seq')
- prefix_owner: int32 [64], replicated, may hold values from 0 to 63, each once
- token_counts: int32 [64, 64], P('seq'), may hold values from 0 to 4, as said below
Outputs:
- attn_out: bfloat16 [8192, 4096], P('seq', 'tensor')
- suffix_key_cache: bfloat16 [8192, 1024], P('seq', 'tensor')
The draws below stay inside these ranges and needn't reach their ends.
Inputs may be any that keep to these rules, and one draw needn't show every extreme that they name: `token_counts`: each row sums to 128; one prefix receives exactly 4 tokens from every sequence index.
All inputs are finite; a program needn't handle non-finite values.
Results may differ from the reference program's by a relative error of at most 0.035.
Values may be sent and summed in bfloat16 or wider, within the bound.
No kernel may reach another device: no remote copies, remote signals or barrier semaphores. Data moves between devices by JAX's collectives and lax.ppermute only.
A program may use at most 64 MiB of HBM per device.

```python
import math
import jax
import jax.numpy as jnp
from jax import lax

MODEL_WIDTH = 4096
QUERY_HEADS = 32
KEY_VALUE_HEADS = 4
HEAD_DIM = 128
SOURCE_TOKENS = 128
PREFIX_LENGTH = 1024
TOKENS = 8192
PREFIX_GROUPS = 64
SUFFIX_SOURCES = 64
CAP = 4
PAIRS = 32


def draw_hidden(key, part):
    random_part = jnp.clip(jax.random.normal(jax.random.fold_in(key, 13), (TOKENS, MODEL_WIDTH), jnp.float32), -6.0, 6.0)
    return random_part.astype(jnp.bfloat16)


def draw_w_query(key, part):
    sampled_values = jnp.clip(jax.random.normal(jax.random.fold_in(key, 11), (MODEL_WIDTH, QUERY_HEADS * HEAD_DIM), jnp.float32), -6.0, 6.0) / math.sqrt(MODEL_WIDTH)
    return sampled_values.astype(jnp.bfloat16)


def draw_key_value_weight(key, part):
    sampled_values = jnp.clip(jax.random.normal(jax.random.fold_in(key, 12), (MODEL_WIDTH, 2 * KEY_VALUE_HEADS * HEAD_DIM), jnp.float32), -6.0, 6.0) / math.sqrt(MODEL_WIDTH)
    return sampled_values.astype(jnp.bfloat16)


def draw_prefix_key_cache(key, part):
    array_shape = (PREFIX_GROUPS, PREFIX_LENGTH, 2 * KEY_VALUE_HEADS * HEAD_DIM)
    values = jax.random.normal(key, array_shape, jnp.float32)
    return values.astype(jnp.bfloat16)


def draw_token_counts(key, part):
    weight = jax.random.randint(jax.random.fold_in(key, 1), (PREFIX_GROUPS,), 1, 9)
    hottest = jax.random.randint(jax.random.fold_in(key, 2), (), 0, PREFIX_GROUPS)
    labels = jnp.arange(PREFIX_GROUPS, dtype=jnp.int32)
    score = jax.random.randint(jax.random.fold_in(key, 3), (SUFFIX_SOURCES, PREFIX_GROUPS), 0, 4096) * weight[None, :]
    score = score * PREFIX_GROUPS + labels[None, :]
    score = jnp.where(labels[None, :] == hottest, 1 << 30, score)
    picked = lax.top_k(score, 2 * PAIRS)[1]
    leading = jax.random.randint(jax.random.fold_in(key, 4), (SUFFIX_SOURCES, PAIRS), 0, CAP + 1)
    leading = jnp.where(jnp.arange(PAIRS)[None, :] == 0, CAP, leading)
    amount = jnp.stack([leading, CAP - leading], axis=2).reshape(SUFFIX_SOURCES, 2 * PAIRS)
    matches = picked[:, :, None] == labels[None, None, :]
    return jnp.sum(jnp.where(matches, amount[:, :, None], 0), axis=1).astype(jnp.int32)


def level_of(rng, extent, pieces, least, largest):
    gain = 1.0
    for axis_at, shards_of in pieces:
        draws = jax.random.uniform(jax.random.fold_in(jax.random.fold_in(rng, 6), axis_at), (shards_of,), jnp.float32, least / len(pieces), largest / len(pieces))
        gain = gain * jnp.repeat(jnp.exp(draws), extent[axis_at] // shards_of).reshape((-1,) + (1,) * (len(extent) - 1 - axis_at))
    return gain


def noise(rng, shape, deviation, most, pieces=(), kind=jnp.bfloat16):
    drawn = deviation * jax.random.normal(rng, shape, jnp.float32)
    if pieces:
        drawn = drawn * level_of(rng, shape, pieces, -0.22, 0.18)
    return jnp.clip(drawn, -most, most).astype(kind)


def setup_inputs(seed: int = 0) -> dict:
    splits = jax.random.split(jax.random.key(seed), 9)
    hidden = draw_hidden(jax.random.fold_in(splits[8], 71), 0)
    norm_gain = jnp.clip(1.0 + 0.1 * jax.random.normal(splits[1], (MODEL_WIDTH,), jnp.float32), 0.5, 1.5).astype(jnp.bfloat16)
    w_query = draw_w_query(jax.random.fold_in(splits[8], 71), 0)
    key_value_weight = draw_key_value_weight(jax.random.fold_in(splits[8], 71), 0)
    w_out = noise(splits[4], (QUERY_HEADS * HEAD_DIM, MODEL_WIDTH), (QUERY_HEADS * HEAD_DIM) ** -0.5, 0.09375, ((0, 8), (1, 64)))
    prefix_key_cache = draw_prefix_key_cache(jax.random.fold_in(splits[8], 71), 0)
    prefix_owner = jax.random.permutation(splits[6], PREFIX_GROUPS).astype(jnp.int32)
    token_counts = draw_token_counts(jax.random.fold_in(splits[8], 71), 0)
    return dict(hidden=hidden, norm_gain=norm_gain, w_query=w_query, key_value_weight=key_value_weight, w_out=w_out, prefix_key_cache=prefix_key_cache, prefix_owner=prefix_owner, token_counts=token_counts)


eps = 1e-06
theta = 5000000.0

def rotate(values, positions):
    half = values.shape[-1] // 2
    frequency = theta ** (-jnp.arange(half, dtype=jnp.float32) * 2.0 / values.shape[-1])
    angle = positions.astype(jnp.float32)[:, None] * frequency[None, :]
    cosine = jnp.cos(angle)[:, None, :]
    sine = jnp.sin(angle)[:, None, :]
    first = values[..., :half]
    second = values[..., half:]
    return jnp.concatenate([first * cosine - second * sine, second * cosine + first * sine], axis=-1)

def layout(counts_row, length):
    ends = jnp.cumsum(counts_row).astype(jnp.int32)
    starts = ends - counts_row
    places = jnp.arange(length, dtype=jnp.int32)
    member = (places[:, None] >= starts[None, :]) & (places[:, None] < ends[None, :])
    labels = jnp.arange(counts_row.shape[0], dtype=jnp.int32)
    prefix_group = lax.optimization_barrier(jnp.sum(jnp.where(member, labels[None, :], 0), axis=1)).astype(jnp.int32)
    offset = places - lax.optimization_barrier(jnp.sum(jnp.where(member, starts[None, :], 0), axis=1)).astype(jnp.int32)
    return (starts, prefix_group, offset)

def attend(query_vectors, keys, values, allowed):
    scores = lax.dot_general(query_vectors, keys, (((1,), (1,)), ((), ())), preferred_element_type=jnp.float32)
    scores = scores * (1.0 / query_vectors.shape[-1] ** 0.5)
    if allowed is not None:
        scores = jnp.where(allowed, scores, -1e+30)
    top = lax.optimization_barrier(jnp.max(scores, axis=1, keepdims=True))
    expo = jnp.exp(scores - top)
    total = lax.optimization_barrier(jnp.sum(expo, axis=1, keepdims=True))
    weights = (expo / total).astype(jnp.bfloat16)
    result = jnp.dot(weights, values, preferred_element_type=jnp.float32)
    return (result, top[:, 0] + jnp.log(total[:, 0]))

def combine(prefix_out, prefix_log, suffix_output, suffix_logsumexp):
    upper = jnp.maximum(prefix_log, suffix_logsumexp)
    left = jnp.exp(prefix_log - upper)[..., None]
    right = jnp.exp(suffix_logsumexp - upper)[..., None]
    mixed = (left * prefix_out.astype(jnp.float32) + right * suffix_output) / (left + right)
    return mixed.astype(jnp.bfloat16)

def reference(hidden, norm_gain, w_query, key_value_weight, w_out, prefix_key_cache, prefix_owner, token_counts):
    token_list = hidden.shape[0]
    group_width = QUERY_HEADS // KEY_VALUE_HEADS
    wide = hidden.astype(jnp.float32)
    normalized_input = (wide * lax.rsqrt(lax.optimization_barrier(jnp.mean(wide * wide, axis=1, keepdims=True)) + eps) * norm_gain.astype(jnp.float32)).astype(jnp.bfloat16)
    starts, prefix_group, offset = jax.vmap(lambda row: layout(row, SOURCE_TOKENS))(token_counts)
    positions = (PREFIX_LENGTH + offset.reshape(-1)).astype(jnp.int32)
    query_vectors = jnp.dot(normalized_input, w_query, preferred_element_type=jnp.float32).reshape(token_list, QUERY_HEADS, HEAD_DIM)
    query_vectors = rotate(query_vectors, positions).astype(jnp.bfloat16)
    key_value_pair = jnp.dot(normalized_input, key_value_weight, preferred_element_type=jnp.float32).reshape(token_list, KEY_VALUE_HEADS, 2, HEAD_DIM)
    rotated = rotate(key_value_pair[:, :, 0], positions)
    key_value_pair = jnp.stack([rotated, key_value_pair[:, :, 1]], axis=2).astype(jnp.bfloat16)
    suffix_key_cache = key_value_pair.reshape(token_list, 2 * KEY_VALUE_HEADS * HEAD_DIM)
    slots = jnp.arange(CAP, dtype=jnp.int32)
    sources = jnp.arange(SUFFIX_SOURCES, dtype=jnp.int32)

    def one_group(carry, group_number):
        out_all, log_all = carry
        cache_entries = lax.dynamic_index_in_dim(prefix_key_cache, prefix_owner[group_number], 0, keepdims=False).reshape(PREFIX_LENGTH, KEY_VALUE_HEADS, 2, HEAD_DIM)
        begin = lax.dynamic_index_in_dim(starts, group_number, 1, keepdims=False)
        amount = lax.dynamic_index_in_dim(token_counts, group_number, 1, keepdims=False)
        valid = (slots[None, :] < amount[:, None]).reshape(-1)
        places = (sources[:, None] * SOURCE_TOKENS + begin[:, None] + slots[None, :]).reshape(-1)
        places = jnp.where(valid, places, 0).astype(jnp.int32)
        picked = jnp.where(valid[:, None, None], query_vectors[places], jnp.zeros((), jnp.bfloat16))
        outs = []
        logs = []
        for head in range(QUERY_HEADS):
            result, logsum = attend(picked[:, head], cache_entries[:, head // group_width, 0], cache_entries[:, head // group_width, 1], None)
            outs.append(result)
            logs.append(logsum)
        result = jnp.stack(outs, axis=1).astype(jnp.bfloat16)
        logsum = jnp.stack(logs, axis=1)
        target = jnp.where(valid, places, token_list).astype(jnp.int32)
        out_all = out_all.at[target].set(result, mode='drop')
        log_all = log_all.at[target].set(logsum, mode='drop')
        return ((out_all, log_all), None)
    init = (jnp.zeros((token_list, QUERY_HEADS, HEAD_DIM), jnp.bfloat16), jnp.zeros((token_list, QUERY_HEADS), jnp.float32))
    (prefix_out, prefix_log), _ = lax.scan(one_group, init, jnp.arange(PREFIX_GROUPS, dtype=jnp.int32))
    places = jnp.arange(SOURCE_TOKENS, dtype=jnp.int32)

    def single_source(args):
        block_query, block_kv, block_group = args
        allowed = (block_group[:, None] == block_group[None, :]) & (places[None, :] <= places[:, None])
        outs = []
        logs = []
        for head in range(QUERY_HEADS):
            result, logsum = attend(block_query[:, head], block_kv[:, head // group_width, 0], block_kv[:, head // group_width, 1], allowed)
            outs.append(result)
            logs.append(logsum)
        return (jnp.stack(outs, axis=1), jnp.stack(logs, axis=1))
    suffix_output, suffix_logsumexp = lax.map(single_source, (query_vectors.reshape(SUFFIX_SOURCES, SOURCE_TOKENS, QUERY_HEADS, HEAD_DIM), key_value_pair.reshape(SUFFIX_SOURCES, SOURCE_TOKENS, KEY_VALUE_HEADS, 2, HEAD_DIM), prefix_group))
    suffix_output = suffix_output.reshape(token_list, QUERY_HEADS, HEAD_DIM)
    suffix_logsumexp = suffix_logsumexp.reshape(token_list, QUERY_HEADS)
    context = combine(prefix_out, prefix_log, suffix_output, suffix_logsumexp).reshape(token_list, QUERY_HEADS * HEAD_DIM)
    attn_out = jnp.dot(context, w_out, preferred_element_type=jnp.float32).astype(jnp.bfloat16)
    return (attn_out, suffix_key_cache)
```

```python
import jax
import jax.numpy as jnp
from jax import lax
from jax.sharding import PartitionSpec as P

HEAD_DIM = 128
PREFIX_LENGTH = 1024


eps = 1e-06
theta = 5000000.0


def rotate(values, positions):
    half = values.shape[-1] // 2
    frequency = theta ** (-jnp.arange(half, dtype=jnp.float32) * 2.0 / values.shape[-1])
    angle = positions.astype(jnp.float32)[:, None] * frequency[None, :]
    cosine = jnp.cos(angle)[:, None, :]
    sine = jnp.sin(angle)[:, None, :]
    first = values[..., :half]
    second = values[..., half:]
    return jnp.concatenate(
        [first * cosine - second * sine, second * cosine + first * sine], axis=-1
    )


def layout(counts_row, length):
    ends = jnp.cumsum(counts_row)
    starts = ends - counts_row
    places = jnp.arange(length, dtype=jnp.int32)
    member = (places[:, None] >= starts[None, :]) & (places[:, None] < ends[None, :])
    labels = jnp.arange(counts_row.shape[0], dtype=jnp.int32)
    prefix_group = jnp.sum(jnp.where(member, labels[None, :], 0), axis=1)
    offset = places - jnp.sum(jnp.where(member, starts[None, :], 0), axis=1)
    return (starts, prefix_group, offset)


def attend(query_vectors, keys, values, allowed):
    scores = lax.dot_general(
        query_vectors, keys, (((1,), (1,)), ((), ())), preferred_element_type=jnp.float32
    )
    scores = scores * (1.0 / query_vectors.shape[-1] ** 0.5)
    if allowed is not None:
        scores = jnp.where(allowed, scores, -1e30)
    top = jnp.max(scores, axis=1, keepdims=True)
    expo = jnp.exp(scores - top)
    total = jnp.sum(expo, axis=1, keepdims=True)
    weights = (expo / total).astype(jnp.bfloat16)
    result = jnp.dot(weights, values, preferred_element_type=jnp.float32)
    return (result, top[:, 0] + jnp.log(total[:, 0]))


def shards(
    hidden,
    norm_gain,
    w_query,
    key_value_weight,
    w_out,
    prefix_key_cache,
    prefix_owner,
    token_counts,
):
    tensor_index = lax.axis_index("tensor")
    tensor_count = lax.axis_size("tensor")
    seq_count = lax.axis_size("seq")
    length = hidden.shape[0]
    head_size = HEAD_DIM
    whole = lax.all_gather(hidden, "tensor", axis=1, tiled=True)
    wide = whole.astype(jnp.float32)
    normalized_input = (
        wide
        * lax.rsqrt(jnp.mean(wide * wide, axis=1, keepdims=True) + eps)
        * norm_gain.astype(jnp.float32)
    ).astype(jnp.bfloat16)
    width_query = w_query.shape[1]
    full_width = key_value_weight.shape[1]
    heads_dev = width_query // head_size
    kv_heads = full_width // (2 * head_size)
    group_full = heads_dev * tensor_count // kv_heads
    kv_local = max(1, heads_dev // group_full)
    kv_start = tensor_index * heads_dev // group_full
    kv_width = kv_local * 2 * head_size
    kv_piece = lax.dynamic_slice_in_dim(key_value_weight, kv_start * 2 * head_size, kv_width, 1)
    packed = jnp.concatenate([w_query, kv_piece, w_out.T], axis=1)
    gathered = lax.all_gather(packed, "seq", axis=0, tiled=True)
    wq_full = gathered[:, :width_query]
    kv_full = gathered[:, width_query : width_query + kv_width]
    wo_cols = gathered[:, width_query + kv_width :]

    def contract(piece):
        return jnp.dot(normalized_input, piece, preferred_element_type=jnp.float32)

    query_vectors = contract(wq_full)
    key_value_pair = contract(kv_full)
    counts = token_counts[0]
    num_groups = counts.shape[0]
    starts, prefix_group, offset = layout(counts, length)
    positions = PREFIX_LENGTH + offset
    query_vectors = rotate(query_vectors.reshape(length, heads_dev, head_size), positions).astype(
        jnp.bfloat16
    )
    pair_blocks = key_value_pair.reshape(length, kv_local, 2, head_size)
    rotated_keys = rotate(pair_blocks[:, :, 0], positions)
    suffix_mine = jnp.stack([rotated_keys, pair_blocks[:, :, 1]], axis=2).astype(jnp.bfloat16)
    share = full_width // tensor_count
    suffix_flat = suffix_mine.reshape(length, kv_width)
    suffix_part = lax.dynamic_slice_in_dim(
        suffix_flat, tensor_index * share - kv_start * 2 * head_size, share, 1
    )
    suffix_keys = suffix_mine[:, :, 0]
    suffix_values = suffix_mine[:, :, 1]
    cache_all = prefix_key_cache[0].reshape(-1, kv_heads, 2, head_size)
    cache_mine = lax.dynamic_slice_in_dim(cache_all, kv_start, kv_local, 1)
    cache_keys = cache_mine[:, :, 0]
    cache_values = cache_mine[:, :, 1]
    group_width = heads_dev // kv_local
    capacity = 2 * length // seq_count
    labels = jnp.arange(num_groups, dtype=jnp.int32)
    owner_match = prefix_owner[None, :] == jnp.arange(seq_count, dtype=jnp.int32)[:, None]
    owner_start = jnp.sum(jnp.where(owner_match, starts[None, :], 0), axis=1)
    owner_count = jnp.sum(jnp.where(owner_match, counts[None, :], 0), axis=1)
    slots = jnp.arange(capacity, dtype=jnp.int32)
    valid = slots[None, :] < owner_count[:, None]
    source_rows = jnp.where(valid, owner_start[:, None] + slots[None, :], 0)
    flat_query = query_vectors.reshape(length, width_query)
    outgoing = jnp.where(valid[:, :, None], flat_query[source_rows], jnp.zeros((), jnp.bfloat16))
    arrived = lax.all_to_all(outgoing, "seq", split_axis=0, concat_axis=0, tiled=True)
    items = arrived.shape[1]
    rows_in = arrived.reshape(seq_count * items, heads_dev, head_size)
    outs = []
    logs = []
    for serve_head in range(heads_dev):
        serve_result, serve_logsum = attend(
            rows_in[:, serve_head],
            cache_keys[:, serve_head // group_width],
            cache_values[:, serve_head // group_width],
            None,
        )
        outs.append(serve_result)
        logs.append(serve_logsum)
    out_block = jnp.stack(outs, axis=1).astype(jnp.bfloat16).reshape(seq_count, items, width_query)
    log_block = jnp.stack(logs, axis=1).reshape(seq_count, items, heads_dev)
    prefix_out = lax.all_to_all(out_block, "seq", split_axis=0, concat_axis=0, tiled=True)
    prefix_log = lax.all_to_all(
        log_block.astype(jnp.bfloat16), "seq", split_axis=0, concat_axis=0, tiled=True
    ).astype(log_block.dtype)
    owner_of_token = jnp.sum(
        jnp.where(prefix_group[:, None] == labels[None, :], prefix_owner[None, :], 0), axis=1
    )
    back_rows = owner_of_token * capacity + offset
    prefix_rows = prefix_out.reshape(seq_count * capacity, heads_dev, head_size)[back_rows]
    prefix_logsum = prefix_log.reshape(seq_count * capacity, heads_dev)[back_rows]
    places = jnp.arange(length, dtype=jnp.int32)
    allowed = (prefix_group[:, None] == prefix_group[None, :]) & (
        places[None, :] <= places[:, None]
    )
    outs = []
    logs = []
    for head in range(heads_dev):
        result, logsum = attend(
            query_vectors[:, head],
            suffix_keys[:, head // group_width],
            suffix_values[:, head // group_width],
            allowed,
        )
        outs.append(result)
        logs.append(logsum)
    suffix_attn = jnp.stack(outs, axis=1)
    suffix_logsum = jnp.stack(logs, axis=1)
    upper = jnp.maximum(prefix_logsum, suffix_logsum)
    left = jnp.exp(prefix_logsum - upper)[..., None]
    right = jnp.exp(suffix_logsum - upper)[..., None]
    context = (
        (left * prefix_rows.astype(jnp.float32) + right * suffix_attn) / (left + right)
    ).astype(jnp.bfloat16)
    context = context.reshape(length, width_query)
    partial_out = lax.dot_general(
        context, wo_cols, (((1,), (1,)), ((), ())), preferred_element_type=jnp.float32
    )
    attn_out = lax.psum_scatter(
        partial_out.astype(jnp.bfloat16), "tensor", scatter_dimension=1, tiled=True
    )
    return (attn_out, suffix_part)


def solution(mesh):
    in_specs = (
        P("seq", "tensor"),
        P(),
        P("seq", "tensor"),
        P("seq", None),
        P("tensor", "seq"),
        P("seq", None, None),
        P(),
        P("seq", None),
    )
    out_specs = (P("seq", "tensor"), P("seq", "tensor"))
    return jax.shard_map(shards, mesh=mesh, in_specs=in_specs, out_specs=out_specs, check_vma=False)
```

```python
import jax
import jax.numpy as jnp
from jax import lax
from jax.sharding import PartitionSpec as P

HEAD_DIM = 128
PREFIX_LENGTH = 1024


eps = 1e-06
theta = 5000000.0


def rotate(values, positions):
    half = values.shape[-1] // 2
    frequency = theta ** (-jnp.arange(half, dtype=jnp.float32) * 2.0 / values.shape[-1])
    angle = positions.astype(jnp.float32)[:, None] * frequency[None, :]
    cosine = jnp.cos(angle)[:, None, :]
    sine = jnp.sin(angle)[:, None, :]
    first = values[..., :half]
    second = values[..., half:]
    return jnp.concatenate(
        [first * cosine - second * sine, second * cosine + first * sine], axis=-1
    )


def layout(counts_row, length):
    ends = jnp.cumsum(counts_row)
    starts = ends - counts_row
    places = jnp.arange(length, dtype=jnp.int32)
    member = (places[:, None] >= starts[None, :]) & (places[:, None] < ends[None, :])
    labels = jnp.arange(counts_row.shape[0], dtype=jnp.int32)
    prefix_group = jnp.sum(jnp.where(member, labels[None, :], 0), axis=1)
    offset = places - jnp.sum(jnp.where(member, starts[None, :], 0), axis=1)
    return (starts, prefix_group, offset)


def attend(query_vectors, keys, values, allowed):
    scores = lax.dot_general(
        query_vectors, keys, (((1,), (1,)), ((), ())), preferred_element_type=jnp.float32
    )
    scores = scores * (1.0 / query_vectors.shape[-1] ** 0.5)
    if allowed is not None:
        scores = jnp.where(allowed, scores, -1e30)
    top = jnp.max(scores, axis=1, keepdims=True)
    expo = jnp.exp(scores - top)
    total = jnp.sum(expo, axis=1, keepdims=True)
    weights = (expo / total).astype(jnp.bfloat16)
    result = jnp.dot(weights, values, preferred_element_type=jnp.float32)
    return (result, top[:, 0] + jnp.log(total[:, 0]))


def shards(
    hidden,
    norm_gain,
    w_query,
    key_value_weight,
    w_out,
    prefix_key_cache,
    prefix_owner,
    token_counts,
):
    tensor_index = lax.axis_index("tensor")
    tensor_count = lax.axis_size("tensor")
    seq_count = lax.axis_size("seq")
    length = hidden.shape[0]
    head_size = HEAD_DIM
    tiles = jnp.broadcast_to(hidden[None], (tensor_count,) + hidden.shape)
    tiles = lax.all_to_all(tiles, "tensor", split_axis=0, concat_axis=0, tiled=True)
    whole = jnp.moveaxis(tiles, 0, 1).reshape(length, tensor_count * hidden.shape[1])
    wide = whole.astype(jnp.float32)
    normalized_input = (
        wide
        * lax.rsqrt(jnp.mean(wide * wide, axis=1, keepdims=True) + eps)
        * norm_gain.astype(jnp.float32)
    ).astype(jnp.bfloat16)
    width_query = w_query.shape[1]
    full_width = key_value_weight.shape[1]
    heads_dev = width_query // head_size
    kv_heads = full_width // (2 * head_size)
    group_full = heads_dev * tensor_count // kv_heads
    kv_local = max(1, heads_dev // group_full)
    kv_start = tensor_index * heads_dev // group_full
    kv_width = kv_local * 2 * head_size
    kv_piece = lax.dynamic_slice_in_dim(key_value_weight, kv_start * 2 * head_size, kv_width, 1)
    packed = jnp.concatenate([w_query, kv_piece, w_out.T], axis=1)
    gathered = lax.all_gather(packed, "seq", axis=0, tiled=True)
    wq_full = gathered[:, :width_query]
    kv_full = gathered[:, width_query : width_query + kv_width]
    wo_cols = gathered[:, width_query + kv_width :]

    def contract(piece):
        return jnp.dot(normalized_input, piece, preferred_element_type=jnp.float32)

    query_vectors = contract(wq_full)
    key_value_pair = contract(kv_full)
    counts = token_counts[0]
    num_groups = counts.shape[0]
    starts, prefix_group, offset = layout(counts, length)
    positions = PREFIX_LENGTH + offset
    query_vectors = rotate(query_vectors.reshape(length, heads_dev, head_size), positions).astype(
        jnp.bfloat16
    )
    pair_blocks = key_value_pair.reshape(length, kv_local, 2, head_size)
    rotated_keys = rotate(pair_blocks[:, :, 0], positions)
    suffix_mine = jnp.stack([rotated_keys, pair_blocks[:, :, 1]], axis=2).astype(jnp.bfloat16)
    share = full_width // tensor_count
    suffix_flat = suffix_mine.reshape(length, kv_width)
    suffix_part = lax.dynamic_slice_in_dim(
        suffix_flat, tensor_index * share - kv_start * 2 * head_size, share, 1
    )
    suffix_keys = suffix_mine[:, :, 0]
    suffix_values = suffix_mine[:, :, 1]
    cache_all = prefix_key_cache[0].reshape(-1, kv_heads, 2, head_size)
    cache_mine = lax.dynamic_slice_in_dim(cache_all, kv_start, kv_local, 1)
    cache_keys = cache_mine[:, :, 0]
    cache_values = cache_mine[:, :, 1]
    group_width = heads_dev // kv_local
    capacity = 2 * length // seq_count
    labels = jnp.arange(num_groups, dtype=jnp.int32)
    owner_match = prefix_owner[None, :] == jnp.arange(seq_count, dtype=jnp.int32)[:, None]
    owner_start = jnp.sum(jnp.where(owner_match, starts[None, :], 0), axis=1)
    owner_count = jnp.sum(jnp.where(owner_match, counts[None, :], 0), axis=1)
    slots = jnp.arange(capacity, dtype=jnp.int32)
    valid = slots[None, :] < owner_count[:, None]
    source_rows = jnp.where(valid, owner_start[:, None] + slots[None, :], 0)
    flat_query = query_vectors.reshape(length, width_query)
    outgoing = jnp.where(valid[:, :, None], flat_query[source_rows], jnp.zeros((), jnp.bfloat16))
    arrived = lax.all_to_all(outgoing, "seq", split_axis=0, concat_axis=0, tiled=True)
    items = arrived.shape[1]
    rows_in = arrived.reshape(seq_count * items, heads_dev, head_size)
    outs = []
    logs = []
    for serve_head in range(heads_dev):
        serve_result, serve_logsum = attend(
            rows_in[:, serve_head],
            cache_keys[:, serve_head // group_width],
            cache_values[:, serve_head // group_width],
            None,
        )
        outs.append(serve_result)
        logs.append(serve_logsum)
    out_block = jnp.stack(outs, axis=1).astype(jnp.bfloat16).reshape(seq_count, items, width_query)
    log_block = jnp.stack(logs, axis=1).reshape(seq_count, items, heads_dev)
    log_row = log_block.astype(jnp.bfloat16).reshape(seq_count, 1, items * heads_dev)
    log_row = jnp.pad(log_row, ((0, 0), (0, 0), (0, width_query - items * heads_dev)))
    back = lax.all_to_all(
        jnp.concatenate([out_block, log_row], axis=1), "seq", split_axis=0, concat_axis=0, tiled=True
    )
    prefix_out = back[:, :items]
    prefix_log = back[:, items, : items * heads_dev].astype(jnp.float32)
    owner_of_token = jnp.sum(
        jnp.where(prefix_group[:, None] == labels[None, :], prefix_owner[None, :], 0), axis=1
    )
    back_rows = owner_of_token * capacity + offset
    prefix_rows = prefix_out.reshape(seq_count * capacity, heads_dev, head_size)[back_rows]
    prefix_logsum = prefix_log.reshape(seq_count * capacity, heads_dev)[back_rows]
    places = jnp.arange(length, dtype=jnp.int32)
    allowed = (prefix_group[:, None] == prefix_group[None, :]) & (
        places[None, :] <= places[:, None]
    )
    outs = []
    logs = []
    for head in range(heads_dev):
        result, logsum = attend(
            query_vectors[:, head],
            suffix_keys[:, head // group_width],
            suffix_values[:, head // group_width],
            allowed,
        )
        outs.append(result)
        logs.append(logsum)
    suffix_attn = jnp.stack(outs, axis=1)
    suffix_logsum = jnp.stack(logs, axis=1)
    upper = jnp.maximum(prefix_logsum, suffix_logsum)
    left = jnp.exp(prefix_logsum - upper)[..., None]
    right = jnp.exp(suffix_logsum - upper)[..., None]
    context = (
        (left * prefix_rows.astype(jnp.float32) + right * suffix_attn) / (left + right)
    ).astype(jnp.bfloat16)
    context = context.reshape(length, width_query)
    partial_out = lax.dot_general(
        context, wo_cols, (((1,), (1,)), ((), ())), preferred_element_type=jnp.float32
    )
    out_width = partial_out.shape[1] // tensor_count
    pieces = partial_out.astype(jnp.bfloat16).reshape(length, tensor_count, out_width)
    pieces = lax.all_to_all(
        jnp.moveaxis(pieces, 1, 0), "tensor", split_axis=0, concat_axis=0, tiled=True
    )
    attn_out = jnp.sum(pieces.astype(jnp.float32), axis=0).astype(jnp.bfloat16)
    return (attn_out, suffix_part)


def solution(mesh):
    in_specs = (
        P("seq", "tensor"),
        P(),
        P("seq", "tensor"),
        P("seq", None),
        P("tensor", "seq"),
        P("seq", None, None),
        P(),
        P("seq", None),
    )
    out_specs = (P("seq", "tensor"), P("seq", "tensor"))
    return jax.shard_map(shards, mesh=mesh, in_specs=in_specs, out_specs=out_specs, check_vma=False)
```

```python
import jax
import jax.numpy as jnp
from jax import lax
from jax.sharding import PartitionSpec as P

HEAD_DIM = 128
PREFIX_LENGTH = 1024


eps = 1e-06
theta = 5000000.0


def rotate(values, positions):
    half = values.shape[-1] // 2
    frequency = theta ** (-jnp.arange(half, dtype=jnp.float32) * 2.0 / values.shape[-1])
    angle = positions.astype(jnp.float32)[:, None] * frequency[None, :]
    cosine = jnp.cos(angle)[:, None, :]
    sine = jnp.sin(angle)[:, None, :]
    first = values[..., :half]
    second = values[..., half:]
    return jnp.concatenate(
        [first * cosine - second * sine, second * cosine + first * sine], axis=-1
    )


def layout(counts_row, length):
    ends = jnp.cumsum(counts_row)
    starts = ends - counts_row
    places = jnp.arange(length, dtype=jnp.int32)
    member = (places[:, None] >= starts[None, :]) & (places[:, None] < ends[None, :])
    labels = jnp.arange(counts_row.shape[0], dtype=jnp.int32)
    prefix_group = jnp.sum(jnp.where(member, labels[None, :], 0), axis=1)
    offset = places - jnp.sum(jnp.where(member, starts[None, :], 0), axis=1)
    return (starts, prefix_group, offset)


def attend(query_vectors, keys, values, allowed):
    scores = lax.dot_general(
        query_vectors, keys, (((1,), (1,)), ((), ())), preferred_element_type=jnp.float32
    )
    scores = scores * (1.0 / query_vectors.shape[-1] ** 0.5)
    if allowed is not None:
        scores = jnp.where(allowed, scores, -1e30)
    top = jnp.max(scores, axis=1, keepdims=True)
    expo = jnp.exp(scores - top)
    total = jnp.sum(expo, axis=1, keepdims=True)
    weights = (expo / total).astype(jnp.bfloat16)
    result = jnp.dot(weights, values, preferred_element_type=jnp.float32)
    return (result, top[:, 0] + jnp.log(total[:, 0]))


Y_CHIPS = 4


def ring(value, count, step):
    rel = [None] * count
    rel[0] = value
    ahead = value
    behind = value
    for k in range(1, count // 2 + 1):
        behind = step(behind, 1)
        rel[(-k) % count] = behind
        if k < count - k:
            ahead = step(ahead, -1)
            rel[k] = ahead
    return rel


def ring_gather(block, axis_name, seq_count):
    z_count = seq_count // Y_CHIPS
    here = lax.axis_index(axis_name)

    def shift(value, dz, dy):
        pairs = []
        for i in range(seq_count):
            z, y = divmod(i, Y_CHIPS)
            pairs.append((i, ((z + dz) % z_count) * Y_CHIPS + (y + dy) % Y_CHIPS))
        return lax.ppermute(value, axis_name, pairs)

    along_y = jnp.stack(ring(block, Y_CHIPS, lambda v, d: shift(v, 0, d)), axis=1)
    along_z = jnp.stack(ring(along_y, z_count, lambda v, d: shift(v, d, 0)), axis=1)
    return along_z.reshape(block.shape[0], -1), here // Y_CHIPS, here % Y_CHIPS


def shards(
    hidden,
    norm_gain,
    w_query,
    key_value_weight,
    w_out,
    prefix_key_cache,
    prefix_owner,
    token_counts,
):
    tensor_index = lax.axis_index("tensor")
    tensor_count = lax.axis_size("tensor")
    seq_count = lax.axis_size("seq")
    length = hidden.shape[0]
    head_size = HEAD_DIM
    tiles = jnp.broadcast_to(hidden[None], (tensor_count,) + hidden.shape)
    tiles = lax.all_to_all(tiles, "tensor", split_axis=0, concat_axis=0, tiled=True)
    whole = jnp.moveaxis(tiles, 0, 1).reshape(length, tensor_count * hidden.shape[1])
    wide = whole.astype(jnp.float32)
    normalized_input = (
        wide
        * lax.rsqrt(jnp.mean(wide * wide, axis=1, keepdims=True) + eps)
        * norm_gain.astype(jnp.float32)
    ).astype(jnp.bfloat16)
    width_query = w_query.shape[1]
    full_width = key_value_weight.shape[1]
    heads_dev = width_query // head_size
    kv_heads = full_width // (2 * head_size)
    group_full = heads_dev * tensor_count // kv_heads
    kv_local = max(1, heads_dev // group_full)
    kv_start = tensor_index * heads_dev // group_full
    kv_width = kv_local * 2 * head_size
    kv_piece = lax.dynamic_slice_in_dim(key_value_weight, kv_start * 2 * head_size, kv_width, 1)
    packed = jnp.concatenate([w_query.T, kv_piece.T, w_out], axis=0)
    gathered, z_at, y_at = ring_gather(packed, "seq", seq_count)
    wq_rows = gathered[:width_query]
    kv_rows = gathered[width_query : width_query + kv_width]
    wo_rel = gathered[width_query + kv_width :]
    z_count = seq_count // Y_CHIPS
    rel_input = normalized_input.reshape(length, z_count, Y_CHIPS, -1)
    rel_input = jnp.roll(jnp.roll(rel_input, -z_at, axis=1), -y_at, axis=2).reshape(length, -1)

    def contract(rows):
        return lax.dot_general(
            rel_input, rows, (((1,), (1,)), ((), ())), preferred_element_type=jnp.float32
        )

    query_vectors = contract(wq_rows)
    key_value_pair = contract(kv_rows)
    counts = token_counts[0]
    num_groups = counts.shape[0]
    starts, prefix_group, offset = layout(counts, length)
    positions = PREFIX_LENGTH + offset
    query_vectors = rotate(query_vectors.reshape(length, heads_dev, head_size), positions).astype(
        jnp.bfloat16
    )
    pair_blocks = key_value_pair.reshape(length, kv_local, 2, head_size)
    rotated_keys = rotate(pair_blocks[:, :, 0], positions)
    suffix_mine = jnp.stack([rotated_keys, pair_blocks[:, :, 1]], axis=2).astype(jnp.bfloat16)
    share = full_width // tensor_count
    suffix_flat = suffix_mine.reshape(length, kv_width)
    suffix_part = lax.dynamic_slice_in_dim(
        suffix_flat, tensor_index * share - kv_start * 2 * head_size, share, 1
    )
    suffix_keys = suffix_mine[:, :, 0]
    suffix_values = suffix_mine[:, :, 1]
    cache_all = prefix_key_cache[0].reshape(-1, kv_heads, 2, head_size)
    cache_mine = lax.dynamic_slice_in_dim(cache_all, kv_start, kv_local, 1)
    cache_keys = cache_mine[:, :, 0]
    cache_values = cache_mine[:, :, 1]
    group_width = heads_dev // kv_local
    capacity = 2 * length // seq_count
    labels = jnp.arange(num_groups, dtype=jnp.int32)
    owner_match = prefix_owner[None, :] == jnp.arange(seq_count, dtype=jnp.int32)[:, None]
    owner_start = jnp.sum(jnp.where(owner_match, starts[None, :], 0), axis=1)
    owner_count = jnp.sum(jnp.where(owner_match, counts[None, :], 0), axis=1)
    slots = jnp.arange(capacity, dtype=jnp.int32)
    valid = slots[None, :] < owner_count[:, None]
    source_rows = jnp.where(valid, owner_start[:, None] + slots[None, :], 0)
    flat_query = query_vectors.reshape(length, width_query)
    outgoing = jnp.where(valid[:, :, None], flat_query[source_rows], jnp.zeros((), jnp.bfloat16))
    arrived = lax.all_to_all(outgoing, "seq", split_axis=0, concat_axis=0, tiled=True)
    items = arrived.shape[1]
    rows_in = arrived.reshape(seq_count * items, heads_dev, head_size)
    outs = []
    logs = []
    for serve_head in range(heads_dev):
        serve_result, serve_logsum = attend(
            rows_in[:, serve_head],
            cache_keys[:, serve_head // group_width],
            cache_values[:, serve_head // group_width],
            None,
        )
        outs.append(serve_result)
        logs.append(serve_logsum)
    out_block = jnp.stack(outs, axis=1).astype(jnp.bfloat16).reshape(seq_count, items, width_query)
    log_block = jnp.stack(logs, axis=1).reshape(seq_count, items, heads_dev)
    log_row = log_block.astype(jnp.bfloat16).reshape(seq_count, 1, items * heads_dev)
    log_row = jnp.pad(log_row, ((0, 0), (0, 0), (0, width_query - items * heads_dev)))
    back = lax.all_to_all(
        jnp.concatenate([out_block, log_row], axis=1), "seq", split_axis=0, concat_axis=0, tiled=True
    )
    prefix_out = back[:, :items]
    prefix_log = back[:, items, : items * heads_dev].astype(jnp.float32)
    owner_of_token = jnp.sum(
        jnp.where(prefix_group[:, None] == labels[None, :], prefix_owner[None, :], 0), axis=1
    )
    back_rows = owner_of_token * capacity + offset
    prefix_rows = prefix_out.reshape(seq_count * capacity, heads_dev, head_size)[back_rows]
    prefix_logsum = prefix_log.reshape(seq_count * capacity, heads_dev)[back_rows]
    places = jnp.arange(length, dtype=jnp.int32)
    allowed = (prefix_group[:, None] == prefix_group[None, :]) & (
        places[None, :] <= places[:, None]
    )
    outs = []
    logs = []
    for head in range(heads_dev):
        result, logsum = attend(
            query_vectors[:, head],
            suffix_keys[:, head // group_width],
            suffix_values[:, head // group_width],
            allowed,
        )
        outs.append(result)
        logs.append(logsum)
    suffix_attn = jnp.stack(outs, axis=1)
    suffix_logsum = jnp.stack(logs, axis=1)
    upper = jnp.maximum(prefix_logsum, suffix_logsum)
    left = jnp.exp(prefix_logsum - upper)[..., None]
    right = jnp.exp(suffix_logsum - upper)[..., None]
    context = (
        (left * prefix_rows.astype(jnp.float32) + right * suffix_attn) / (left + right)
    ).astype(jnp.bfloat16)
    context = context.reshape(length, width_query)
    partial_out = jnp.dot(context, wo_rel, preferred_element_type=jnp.float32)
    partial_out = partial_out.reshape(length, z_count, Y_CHIPS, -1)
    partial_out = jnp.roll(jnp.roll(partial_out, z_at, axis=1), y_at, axis=2).reshape(length, -1)
    out_width = partial_out.shape[1] // tensor_count
    pieces = partial_out.astype(jnp.bfloat16).reshape(length, tensor_count, out_width)
    pieces = lax.all_to_all(
        jnp.moveaxis(pieces, 1, 0), "tensor", split_axis=0, concat_axis=0, tiled=True
    )
    attn_out = jnp.sum(pieces.astype(jnp.float32), axis=0).astype(jnp.bfloat16)
    return (attn_out, suffix_part)


def solution(mesh):
    in_specs = (
        P("seq", "tensor"),
        P(),
        P("seq", "tensor"),
        P("seq", None),
        P("tensor", "seq"),
        P("seq", None, None),
        P(),
        P("seq", None),
    )
    out_specs = (P("seq", "tensor"), P("seq", "tensor"))
    return jax.shard_map(shards, mesh=mesh, in_specs=in_specs, out_specs=out_specs, check_vma=False)
```

```python
import jax
import jax.numpy as jnp
from jax import lax
from jax.sharding import PartitionSpec as P

HEAD_DIM = 128
PREFIX_LENGTH = 1024


eps = 1e-06
theta = 5000000.0


def rotate(values, positions):
    half = values.shape[-1] // 2
    frequency = theta ** (-jnp.arange(half, dtype=jnp.float32) * 2.0 / values.shape[-1])
    angle = positions.astype(jnp.float32)[:, None] * frequency[None, :]
    cosine = jnp.cos(angle)[:, None, :]
    sine = jnp.sin(angle)[:, None, :]
    first = values[..., :half]
    second = values[..., half:]
    return jnp.concatenate(
        [first * cosine - second * sine, second * cosine + first * sine], axis=-1
    )


def layout(counts_row, length):
    ends = jnp.cumsum(counts_row)
    starts = ends - counts_row
    places = jnp.arange(length, dtype=jnp.int32)
    member = (places[:, None] >= starts[None, :]) & (places[:, None] < ends[None, :])
    labels = jnp.arange(counts_row.shape[0], dtype=jnp.int32)
    prefix_group = jnp.sum(jnp.where(member, labels[None, :], 0), axis=1)
    offset = places - jnp.sum(jnp.where(member, starts[None, :], 0), axis=1)
    return (starts, prefix_group, offset)


def attend(query_vectors, keys, values, allowed):
    scores = lax.dot_general(
        query_vectors, keys, (((1,), (1,)), ((), ())), preferred_element_type=jnp.float32
    )
    scores = scores * (1.0 / query_vectors.shape[-1] ** 0.5)
    if allowed is not None:
        scores = jnp.where(allowed, scores, -1e30)
    top = jnp.max(scores, axis=1, keepdims=True)
    expo = jnp.exp(scores - top)
    total = jnp.sum(expo, axis=1, keepdims=True)
    weights = (expo / total).astype(jnp.bfloat16)
    result = jnp.dot(weights, values, preferred_element_type=jnp.float32)
    return (result, top[:, 0] + jnp.log(total[:, 0]))


Y_CHIPS = 4


def ring(value, count, step):
    rel = [None] * count
    rel[0] = value
    ahead = value
    behind = value
    for k in range(1, count // 2 + 1):
        if k < count - k:
            behind = step(behind, 1)
            rel[(-k) % count] = behind
            ahead = step(ahead, -1)
            rel[k] = ahead
        else:
            half = value.shape[0] // 2
            rel[k] = jnp.concatenate([step(behind[:half], 1), step(ahead[half:], -1)], axis=0)
    return rel


def ring_gather(y_first, z_first, axis_name, seq_count):
    z_count = seq_count // Y_CHIPS
    here = lax.axis_index(axis_name)

    def shift(value, dz, dy):
        pairs = []
        for i in range(seq_count):
            z, y = divmod(i, Y_CHIPS)
            pairs.append((i, ((z + dz) % z_count) * Y_CHIPS + (y + dy) % Y_CHIPS))
        return lax.ppermute(value, axis_name, pairs)

    def on_y(v, d):
        return shift(v, 0, d)

    def on_z(v, d):
        return shift(v, d, 0)

    part_a = jnp.stack(ring(jnp.stack(ring(y_first, Y_CHIPS, on_y), axis=1), z_count, on_z), axis=1)
    part_b = jnp.stack(ring(jnp.stack(ring(z_first, z_count, on_z), axis=1), Y_CHIPS, on_y), axis=2)
    rows_a = part_a.reshape(y_first.shape[0], -1)
    rows_b = part_b.reshape(z_first.shape[0], -1)
    return rows_a, rows_b, here // Y_CHIPS, here % Y_CHIPS


def shards(
    hidden,
    norm_gain,
    w_query,
    key_value_weight,
    w_out,
    prefix_key_cache,
    prefix_owner,
    token_counts,
):
    tensor_index = lax.axis_index("tensor")
    tensor_count = lax.axis_size("tensor")
    seq_count = lax.axis_size("seq")
    length = hidden.shape[0]
    head_size = HEAD_DIM
    tiles = jnp.broadcast_to(hidden[None], (tensor_count,) + hidden.shape)
    tiles = lax.all_to_all(tiles, "tensor", split_axis=0, concat_axis=0, tiled=True)
    whole = jnp.moveaxis(tiles, 0, 1).reshape(length, tensor_count * hidden.shape[1])
    wide = whole.astype(jnp.float32)
    normalized_input = (
        wide
        * lax.rsqrt(jnp.mean(wide * wide, axis=1, keepdims=True) + eps)
        * norm_gain.astype(jnp.float32)
    ).astype(jnp.bfloat16)
    width_query = w_query.shape[1]
    full_width = key_value_weight.shape[1]
    heads_dev = width_query // head_size
    kv_heads = full_width // (2 * head_size)
    group_full = heads_dev * tensor_count // kv_heads
    kv_local = max(1, heads_dev // group_full)
    kv_start = tensor_index * heads_dev // group_full
    kv_width = kv_local * 2 * head_size
    kv_piece = lax.dynamic_slice_in_dim(key_value_weight, kv_start * 2 * head_size, kv_width, 1)
    packed = jnp.concatenate([kv_piece.T, w_out], axis=0)
    wq_rows, rest, z_at, y_at = ring_gather(w_query.T, packed, "seq", seq_count)
    kv_rows = rest[:kv_width]
    wo_rel = rest[kv_width:]
    z_count = seq_count // Y_CHIPS
    rel_input = normalized_input.reshape(length, z_count, Y_CHIPS, -1)
    rel_input = jnp.roll(jnp.roll(rel_input, -z_at, axis=1), -y_at, axis=2).reshape(length, -1)

    def contract(rows):
        return lax.dot_general(
            rel_input, rows, (((1,), (1,)), ((), ())), preferred_element_type=jnp.float32
        )

    query_vectors = contract(wq_rows)
    key_value_pair = contract(kv_rows)
    counts = token_counts[0]
    num_groups = counts.shape[0]
    starts, prefix_group, offset = layout(counts, length)
    positions = PREFIX_LENGTH + offset
    query_vectors = rotate(query_vectors.reshape(length, heads_dev, head_size), positions).astype(
        jnp.bfloat16
    )
    pair_blocks = key_value_pair.reshape(length, kv_local, 2, head_size)
    rotated_keys = rotate(pair_blocks[:, :, 0], positions)
    suffix_mine = jnp.stack([rotated_keys, pair_blocks[:, :, 1]], axis=2).astype(jnp.bfloat16)
    share = full_width // tensor_count
    suffix_flat = suffix_mine.reshape(length, kv_width)
    suffix_part = lax.dynamic_slice_in_dim(
        suffix_flat, tensor_index * share - kv_start * 2 * head_size, share, 1
    )
    suffix_keys = suffix_mine[:, :, 0]
    suffix_values = suffix_mine[:, :, 1]
    cache_all = prefix_key_cache[0].reshape(-1, kv_heads, 2, head_size)
    cache_mine = lax.dynamic_slice_in_dim(cache_all, kv_start, kv_local, 1)
    cache_keys = cache_mine[:, :, 0]
    cache_values = cache_mine[:, :, 1]
    group_width = heads_dev // kv_local
    capacity = 2 * length // seq_count
    labels = jnp.arange(num_groups, dtype=jnp.int32)
    owner_match = prefix_owner[None, :] == jnp.arange(seq_count, dtype=jnp.int32)[:, None]
    owner_start = jnp.sum(jnp.where(owner_match, starts[None, :], 0), axis=1)
    owner_count = jnp.sum(jnp.where(owner_match, counts[None, :], 0), axis=1)
    slots = jnp.arange(capacity, dtype=jnp.int32)
    valid = slots[None, :] < owner_count[:, None]
    source_rows = jnp.where(valid, owner_start[:, None] + slots[None, :], 0)
    flat_query = query_vectors.reshape(length, width_query)
    outgoing = jnp.where(valid[:, :, None], flat_query[source_rows], jnp.zeros((), jnp.bfloat16))
    arrived = lax.all_to_all(outgoing, "seq", split_axis=0, concat_axis=0, tiled=True)
    items = arrived.shape[1]
    rows_in = arrived.reshape(seq_count * items, heads_dev, head_size)
    outs = []
    logs = []
    for serve_head in range(heads_dev):
        serve_result, serve_logsum = attend(
            rows_in[:, serve_head],
            cache_keys[:, serve_head // group_width],
            cache_values[:, serve_head // group_width],
            None,
        )
        outs.append(serve_result)
        logs.append(serve_logsum)
    out_block = jnp.stack(outs, axis=1).astype(jnp.bfloat16).reshape(seq_count, items, width_query)
    log_block = jnp.stack(logs, axis=1).reshape(seq_count, items, heads_dev)
    log_row = log_block.astype(jnp.bfloat16).reshape(seq_count, 1, items * heads_dev)
    log_row = jnp.pad(log_row, ((0, 0), (0, 0), (0, width_query - items * heads_dev)))
    back = lax.all_to_all(
        jnp.concatenate([out_block, log_row], axis=1), "seq", split_axis=0, concat_axis=0, tiled=True
    )
    prefix_out = back[:, :items]
    prefix_log = back[:, items, : items * heads_dev].astype(jnp.float32)
    owner_of_token = jnp.sum(
        jnp.where(prefix_group[:, None] == labels[None, :], prefix_owner[None, :], 0), axis=1
    )
    back_rows = owner_of_token * capacity + offset
    prefix_rows = prefix_out.reshape(seq_count * capacity, heads_dev, head_size)[back_rows]
    prefix_logsum = prefix_log.reshape(seq_count * capacity, heads_dev)[back_rows]
    places = jnp.arange(length, dtype=jnp.int32)
    allowed = (prefix_group[:, None] == prefix_group[None, :]) & (
        places[None, :] <= places[:, None]
    )
    outs = []
    logs = []
    for head in range(heads_dev):
        result, logsum = attend(
            query_vectors[:, head],
            suffix_keys[:, head // group_width],
            suffix_values[:, head // group_width],
            allowed,
        )
        outs.append(result)
        logs.append(logsum)
    suffix_attn = jnp.stack(outs, axis=1)
    suffix_logsum = jnp.stack(logs, axis=1)
    upper = jnp.maximum(prefix_logsum, suffix_logsum)
    left = jnp.exp(prefix_logsum - upper)[..., None]
    right = jnp.exp(suffix_logsum - upper)[..., None]
    context = (
        (left * prefix_rows.astype(jnp.float32) + right * suffix_attn) / (left + right)
    ).astype(jnp.bfloat16)
    context = context.reshape(length, width_query)
    partial_out = jnp.dot(context, wo_rel, preferred_element_type=jnp.float32)
    partial_out = partial_out.reshape(length, z_count, Y_CHIPS, -1)
    partial_out = jnp.roll(jnp.roll(partial_out, z_at, axis=1), y_at, axis=2).reshape(length, -1)
    out_width = partial_out.shape[1] // tensor_count
    pieces = partial_out.astype(jnp.bfloat16).reshape(length, tensor_count, out_width)
    pieces = lax.all_to_all(
        jnp.moveaxis(pieces, 1, 0), "tensor", split_axis=0, concat_axis=0, tiled=True
    )
    attn_out = jnp.sum(pieces.astype(jnp.float32), axis=0).astype(jnp.bfloat16)
    return (attn_out, suffix_part)


def solution(mesh):
    in_specs = (
        P("seq", "tensor"),
        P(),
        P("seq", "tensor"),
        P("seq", None),
        P("tensor", "seq"),
        P("seq", None, None),
        P(),
        P("seq", None),
    )
    out_specs = (P("seq", "tensor"), P("seq", "tensor"))
    return jax.shard_map(shards, mesh=mesh, in_specs=in_specs, out_specs=out_specs, check_vma=False)
```

```python
import jax
import jax.numpy as jnp
from jax import lax
from jax.sharding import PartitionSpec as P

HEAD_DIM = 128
PREFIX_LENGTH = 1024


eps = 1e-06
theta = 5000000.0


def rotate(values, positions):
    half = values.shape[-1] // 2
    frequency = theta ** (-jnp.arange(half, dtype=jnp.float32) * 2.0 / values.shape[-1])
    angle = positions.astype(jnp.float32)[:, None] * frequency[None, :]
    cosine = jnp.cos(angle)[:, None, :]
    sine = jnp.sin(angle)[:, None, :]
    first = values[..., :half]
    second = values[..., half:]
    return jnp.concatenate(
        [first * cosine - second * sine, second * cosine + first * sine], axis=-1
    )


def layout(counts_row, length):
    ends = jnp.cumsum(counts_row)
    starts = ends - counts_row
    places = jnp.arange(length, dtype=jnp.int32)
    member = (places[:, None] >= starts[None, :]) & (places[:, None] < ends[None, :])
    labels = jnp.arange(counts_row.shape[0], dtype=jnp.int32)
    prefix_group = jnp.sum(jnp.where(member, labels[None, :], 0), axis=1)
    offset = places - jnp.sum(jnp.where(member, starts[None, :], 0), axis=1)
    return (starts, prefix_group, offset)


def attend(query_vectors, keys, values, allowed):
    scores = lax.dot_general(
        query_vectors, keys, (((1,), (1,)), ((), ())), preferred_element_type=jnp.float32
    )
    scores = scores * (1.0 / query_vectors.shape[-1] ** 0.5)
    if allowed is not None:
        scores = jnp.where(allowed, scores, -1e30)
    top = jnp.max(scores, axis=1, keepdims=True)
    expo = jnp.exp(scores - top)
    total = jnp.sum(expo, axis=1, keepdims=True)
    weights = (expo / total).astype(jnp.bfloat16)
    result = jnp.dot(weights, values, preferred_element_type=jnp.float32)
    return (result, top[:, 0] + jnp.log(total[:, 0]))


Y_CHIPS = 4


def ring(value, count, step):
    rel = [None] * count
    rel[0] = value
    ahead = value
    behind = value
    for k in range(1, count // 2 + 1):
        behind = step(behind, 1)
        rel[(-k) % count] = behind
        if k < count - k:
            ahead = step(ahead, -1)
            rel[k] = ahead
    return rel


def ring_gather(block, axis_name, seq_count):
    z_count = seq_count // Y_CHIPS
    here = lax.axis_index(axis_name)

    def shift(value, dz, dy):
        pairs = []
        for i in range(seq_count):
            z, y = divmod(i, Y_CHIPS)
            pairs.append((i, ((z + dz) % z_count) * Y_CHIPS + (y + dy) % Y_CHIPS))
        return lax.ppermute(value, axis_name, pairs)

    along_y = jnp.stack(ring(block, Y_CHIPS, lambda v, d: shift(v, 0, d)), axis=1)
    along_z = jnp.stack(ring(along_y, z_count, lambda v, d: shift(v, d, 0)), axis=1)
    return along_z.reshape(block.shape[0], -1), here // Y_CHIPS, here % Y_CHIPS


def shards(
    hidden,
    norm_gain,
    w_query,
    key_value_weight,
    w_out,
    prefix_key_cache,
    prefix_owner,
    token_counts,
):
    tensor_index = lax.axis_index("tensor")
    tensor_count = lax.axis_size("tensor")
    seq_count = lax.axis_size("seq")
    length = hidden.shape[0]
    head_size = HEAD_DIM
    tiles = jnp.broadcast_to(hidden[None], (tensor_count,) + hidden.shape)
    tiles = lax.all_to_all(tiles, "tensor", split_axis=0, concat_axis=0, tiled=True)
    whole = jnp.moveaxis(tiles, 0, 1).reshape(length, tensor_count * hidden.shape[1])
    wide = whole.astype(jnp.float32)
    normalized_input = (
        wide
        * lax.rsqrt(jnp.mean(wide * wide, axis=1, keepdims=True) + eps)
        * norm_gain.astype(jnp.float32)
    ).astype(jnp.bfloat16)
    width_query = w_query.shape[1]
    full_width = key_value_weight.shape[1]
    heads_dev = width_query // head_size
    kv_heads = full_width // (2 * head_size)
    group_full = heads_dev * tensor_count // kv_heads
    kv_local = max(1, heads_dev // group_full)
    kv_start = tensor_index * heads_dev // group_full
    kv_width = kv_local * 2 * head_size
    kv_piece = lax.dynamic_slice_in_dim(key_value_weight, kv_start * 2 * head_size, kv_width, 1)
    packed = jnp.concatenate([w_query.T, kv_piece.T], axis=0)
    gathered, z_at, y_at = ring_gather(packed, "seq", seq_count)
    wq_rows = gathered[:width_query]
    kv_rows = gathered[width_query:]
    z_count = seq_count // Y_CHIPS
    rel_input = normalized_input.reshape(length, z_count, Y_CHIPS, -1)
    rel_input = jnp.roll(jnp.roll(rel_input, -z_at, axis=1), -y_at, axis=2).reshape(length, -1)

    def contract(rows):
        return lax.dot_general(
            rel_input, rows, (((1,), (1,)), ((), ())), preferred_element_type=jnp.float32
        )

    query_vectors = contract(wq_rows)
    key_value_pair = contract(kv_rows)
    counts = token_counts[0]
    num_groups = counts.shape[0]
    starts, prefix_group, offset = layout(counts, length)
    positions = PREFIX_LENGTH + offset
    query_vectors = rotate(query_vectors.reshape(length, heads_dev, head_size), positions).astype(
        jnp.bfloat16
    )
    pair_blocks = key_value_pair.reshape(length, kv_local, 2, head_size)
    rotated_keys = rotate(pair_blocks[:, :, 0], positions)
    suffix_mine = jnp.stack([rotated_keys, pair_blocks[:, :, 1]], axis=2).astype(jnp.bfloat16)
    share = full_width // tensor_count
    suffix_flat = suffix_mine.reshape(length, kv_width)
    suffix_part = lax.dynamic_slice_in_dim(
        suffix_flat, tensor_index * share - kv_start * 2 * head_size, share, 1
    )
    suffix_keys = suffix_mine[:, :, 0]
    suffix_values = suffix_mine[:, :, 1]
    cache_all = prefix_key_cache[0].reshape(-1, kv_heads, 2, head_size)
    cache_mine = lax.dynamic_slice_in_dim(cache_all, kv_start, kv_local, 1)
    cache_keys = cache_mine[:, :, 0]
    cache_values = cache_mine[:, :, 1]
    group_width = heads_dev // kv_local
    capacity = 2 * length // seq_count
    labels = jnp.arange(num_groups, dtype=jnp.int32)
    owner_match = prefix_owner[None, :] == jnp.arange(seq_count, dtype=jnp.int32)[:, None]
    owner_start = jnp.sum(jnp.where(owner_match, starts[None, :], 0), axis=1)
    owner_count = jnp.sum(jnp.where(owner_match, counts[None, :], 0), axis=1)
    slots = jnp.arange(capacity, dtype=jnp.int32)
    valid = slots[None, :] < owner_count[:, None]
    source_rows = jnp.where(valid, owner_start[:, None] + slots[None, :], 0)
    flat_query = query_vectors.reshape(length, width_query)
    outgoing = jnp.where(valid[:, :, None], flat_query[source_rows], jnp.zeros((), jnp.bfloat16))
    outgoing, wo_block = lax.optimization_barrier((outgoing, w_out))
    wo_rel, _, _ = ring_gather(wo_block, "seq", seq_count)
    arrived = lax.all_to_all(outgoing, "seq", split_axis=0, concat_axis=0, tiled=True)
    items = arrived.shape[1]
    rows_in = arrived.reshape(seq_count * items, heads_dev, head_size)
    outs = []
    logs = []
    for serve_head in range(heads_dev):
        serve_result, serve_logsum = attend(
            rows_in[:, serve_head],
            cache_keys[:, serve_head // group_width],
            cache_values[:, serve_head // group_width],
            None,
        )
        outs.append(serve_result)
        logs.append(serve_logsum)
    out_block = jnp.stack(outs, axis=1).astype(jnp.bfloat16).reshape(seq_count, items, width_query)
    log_block = jnp.stack(logs, axis=1).reshape(seq_count, items, heads_dev)
    log_row = log_block.astype(jnp.bfloat16).reshape(seq_count, 1, items * heads_dev)
    log_row = jnp.pad(log_row, ((0, 0), (0, 0), (0, width_query - items * heads_dev)))
    back = lax.all_to_all(
        jnp.concatenate([out_block, log_row], axis=1), "seq", split_axis=0, concat_axis=0, tiled=True
    )
    prefix_out = back[:, :items]
    prefix_log = back[:, items, : items * heads_dev].astype(jnp.float32)
    owner_of_token = jnp.sum(
        jnp.where(prefix_group[:, None] == labels[None, :], prefix_owner[None, :], 0), axis=1
    )
    back_rows = owner_of_token * capacity + offset
    prefix_rows = prefix_out.reshape(seq_count * capacity, heads_dev, head_size)[back_rows]
    prefix_logsum = prefix_log.reshape(seq_count * capacity, heads_dev)[back_rows]
    places = jnp.arange(length, dtype=jnp.int32)
    allowed = (prefix_group[:, None] == prefix_group[None, :]) & (
        places[None, :] <= places[:, None]
    )
    outs = []
    logs = []
    for head in range(heads_dev):
        result, logsum = attend(
            query_vectors[:, head],
            suffix_keys[:, head // group_width],
            suffix_values[:, head // group_width],
            allowed,
        )
        outs.append(result)
        logs.append(logsum)
    suffix_attn = jnp.stack(outs, axis=1)
    suffix_logsum = jnp.stack(logs, axis=1)
    upper = jnp.maximum(prefix_logsum, suffix_logsum)
    left = jnp.exp(prefix_logsum - upper)[..., None]
    right = jnp.exp(suffix_logsum - upper)[..., None]
    context = (
        (left * prefix_rows.astype(jnp.float32) + right * suffix_attn) / (left + right)
    ).astype(jnp.bfloat16)
    context = context.reshape(length, width_query)
    partial_out = jnp.dot(context, wo_rel, preferred_element_type=jnp.float32)
    partial_out = partial_out.reshape(length, z_count, Y_CHIPS, -1)
    partial_out = jnp.roll(jnp.roll(partial_out, z_at, axis=1), y_at, axis=2).reshape(length, -1)
    out_width = partial_out.shape[1] // tensor_count
    pieces = partial_out.astype(jnp.bfloat16).reshape(length, tensor_count, out_width)
    pieces = lax.all_to_all(
        jnp.moveaxis(pieces, 1, 0), "tensor", split_axis=0, concat_axis=0, tiled=True
    )
    attn_out = jnp.sum(pieces.astype(jnp.float32), axis=0).astype(jnp.bfloat16)
    return (attn_out, suffix_part)


def solution(mesh):
    in_specs = (
        P("seq", "tensor"),
        P(),
        P("seq", "tensor"),
        P("seq", None),
        P("tensor", "seq"),
        P("seq", None, None),
        P(),
        P("seq", None),
    )
    out_specs = (P("seq", "tensor"), P("seq", "tensor"))
    return jax.shard_map(shards, mesh=mesh, in_specs=in_specs, out_specs=out_specs, check_vma=False)
```

```python
import jax
import jax.numpy as jnp
from jax import lax
from jax.sharding import PartitionSpec as P

HEAD_DIM = 128
PREFIX_LENGTH = 1024


eps = 1e-06
theta = 5000000.0


def rotate(values, positions):
    half = values.shape[-1] // 2
    frequency = theta ** (-jnp.arange(half, dtype=jnp.float32) * 2.0 / values.shape[-1])
    angle = positions.astype(jnp.float32)[:, None] * frequency[None, :]
    cosine = jnp.cos(angle)[:, None, :]
    sine = jnp.sin(angle)[:, None, :]
    first = values[..., :half]
    second = values[..., half:]
    return jnp.concatenate(
        [first * cosine - second * sine, second * cosine + first * sine], axis=-1
    )


def layout(counts_row, length):
    ends = jnp.cumsum(counts_row)
    starts = ends - counts_row
    places = jnp.arange(length, dtype=jnp.int32)
    member = (places[:, None] >= starts[None, :]) & (places[:, None] < ends[None, :])
    labels = jnp.arange(counts_row.shape[0], dtype=jnp.int32)
    prefix_group = jnp.sum(jnp.where(member, labels[None, :], 0), axis=1)
    offset = places - jnp.sum(jnp.where(member, starts[None, :], 0), axis=1)
    return (starts, prefix_group, offset)


def attend(query_vectors, keys, values, allowed):
    scores = lax.dot_general(
        query_vectors, keys, (((1,), (1,)), ((), ())), preferred_element_type=jnp.float32
    )
    scores = scores * (1.0 / query_vectors.shape[-1] ** 0.5)
    if allowed is not None:
        scores = jnp.where(allowed, scores, -1e30)
    top = jnp.max(scores, axis=1, keepdims=True)
    expo = jnp.exp(scores - top)
    total = jnp.sum(expo, axis=1, keepdims=True)
    weights = (expo / total).astype(jnp.bfloat16)
    result = jnp.dot(weights, values, preferred_element_type=jnp.float32)
    return (result, top[:, 0] + jnp.log(total[:, 0]))


Y_CHIPS = 4


def ring(value, count, step):
    rel = [None] * count
    rel[0] = value
    ahead = value
    behind = value
    for k in range(1, count // 2 + 1):
        behind = step(behind, 1)
        rel[(-k) % count] = behind
        if k < count - k:
            ahead = step(ahead, -1)
            rel[k] = ahead
    return rel


def ring_gather(block, axis_name, seq_count):
    z_count = seq_count // Y_CHIPS
    here = lax.axis_index(axis_name)

    def shift(value, dz, dy):
        pairs = []
        for i in range(seq_count):
            z, y = divmod(i, Y_CHIPS)
            pairs.append((i, ((z + dz) % z_count) * Y_CHIPS + (y + dy) % Y_CHIPS))
        return lax.ppermute(value, axis_name, pairs)

    along_y = jnp.stack(ring(block, Y_CHIPS, lambda v, d: shift(v, 0, d)), axis=1)
    along_z = jnp.stack(ring(along_y, z_count, lambda v, d: shift(v, d, 0)), axis=1)
    return along_z.reshape(block.shape[0], -1), here // Y_CHIPS, here % Y_CHIPS


def shards(
    hidden,
    norm_gain,
    w_query,
    key_value_weight,
    w_out,
    prefix_key_cache,
    prefix_owner,
    token_counts,
):
    tensor_index = lax.axis_index("tensor")
    tensor_count = lax.axis_size("tensor")
    seq_count = lax.axis_size("seq")
    length = hidden.shape[0]
    head_size = HEAD_DIM
    tiles = jnp.broadcast_to(hidden[None], (tensor_count,) + hidden.shape)
    tiles = lax.all_to_all(tiles, "tensor", split_axis=0, concat_axis=0, tiled=True)
    whole = jnp.moveaxis(tiles, 0, 1).reshape(length, tensor_count * hidden.shape[1])
    wide = whole.astype(jnp.float32)
    normalized_input = (
        wide
        * lax.rsqrt(jnp.mean(wide * wide, axis=1, keepdims=True) + eps)
        * norm_gain.astype(jnp.float32)
    ).astype(jnp.bfloat16)
    width_query = w_query.shape[1]
    full_width = key_value_weight.shape[1]
    heads_dev = width_query // head_size
    kv_heads = full_width // (2 * head_size)
    group_full = heads_dev * tensor_count // kv_heads
    kv_local = max(1, heads_dev // group_full)
    kv_start = tensor_index * heads_dev // group_full
    kv_width = kv_local * 2 * head_size
    kv_piece = lax.dynamic_slice_in_dim(key_value_weight, kv_start * 2 * head_size, kv_width, 1)
    wo_full = lax.all_gather(w_out, "seq", axis=1, tiled=True)
    packed = jnp.concatenate([w_query.T, kv_piece.T], axis=0)
    gathered, z_at, y_at = ring_gather(packed, "seq", seq_count)
    wq_rows = gathered[:width_query]
    kv_rows = gathered[width_query:]
    z_count = seq_count // Y_CHIPS
    rel_input = normalized_input.reshape(length, z_count, Y_CHIPS, -1)
    rel_input = jnp.roll(jnp.roll(rel_input, -z_at, axis=1), -y_at, axis=2).reshape(length, -1)

    def contract(rows):
        return lax.dot_general(
            rel_input, rows, (((1,), (1,)), ((), ())), preferred_element_type=jnp.float32
        )

    query_vectors = contract(wq_rows)
    key_value_pair = contract(kv_rows)
    counts = token_counts[0]
    num_groups = counts.shape[0]
    starts, prefix_group, offset = layout(counts, length)
    positions = PREFIX_LENGTH + offset
    query_vectors = rotate(query_vectors.reshape(length, heads_dev, head_size), positions).astype(
        jnp.bfloat16
    )
    pair_blocks = key_value_pair.reshape(length, kv_local, 2, head_size)
    rotated_keys = rotate(pair_blocks[:, :, 0], positions)
    suffix_mine = jnp.stack([rotated_keys, pair_blocks[:, :, 1]], axis=2).astype(jnp.bfloat16)
    share = full_width // tensor_count
    suffix_flat = suffix_mine.reshape(length, kv_width)
    suffix_part = lax.dynamic_slice_in_dim(
        suffix_flat, tensor_index * share - kv_start * 2 * head_size, share, 1
    )
    suffix_keys = suffix_mine[:, :, 0]
    suffix_values = suffix_mine[:, :, 1]
    cache_all = prefix_key_cache[0].reshape(-1, kv_heads, 2, head_size)
    cache_mine = lax.dynamic_slice_in_dim(cache_all, kv_start, kv_local, 1)
    cache_keys = cache_mine[:, :, 0]
    cache_values = cache_mine[:, :, 1]
    group_width = heads_dev // kv_local
    capacity = 2 * length // seq_count
    labels = jnp.arange(num_groups, dtype=jnp.int32)
    owner_match = prefix_owner[None, :] == jnp.arange(seq_count, dtype=jnp.int32)[:, None]
    owner_start = jnp.sum(jnp.where(owner_match, starts[None, :], 0), axis=1)
    owner_count = jnp.sum(jnp.where(owner_match, counts[None, :], 0), axis=1)
    slots = jnp.arange(capacity, dtype=jnp.int32)
    valid = slots[None, :] < owner_count[:, None]
    source_rows = jnp.where(valid, owner_start[:, None] + slots[None, :], 0)
    flat_query = query_vectors.reshape(length, width_query)
    outgoing = jnp.where(valid[:, :, None], flat_query[source_rows], jnp.zeros((), jnp.bfloat16))
    arrived = lax.all_to_all(outgoing, "seq", split_axis=0, concat_axis=0, tiled=True)
    items = arrived.shape[1]
    rows_in = arrived.reshape(seq_count * items, heads_dev, head_size)
    outs = []
    logs = []
    for serve_head in range(heads_dev):
        serve_result, serve_logsum = attend(
            rows_in[:, serve_head],
            cache_keys[:, serve_head // group_width],
            cache_values[:, serve_head // group_width],
            None,
        )
        outs.append(serve_result)
        logs.append(serve_logsum)
    out_block = jnp.stack(outs, axis=1).astype(jnp.bfloat16).reshape(seq_count, items, width_query)
    log_block = jnp.stack(logs, axis=1).reshape(seq_count, items, heads_dev)
    log_row = log_block.astype(jnp.bfloat16).reshape(seq_count, 1, items * heads_dev)
    log_row = jnp.pad(log_row, ((0, 0), (0, 0), (0, width_query - items * heads_dev)))
    back = lax.all_to_all(
        jnp.concatenate([out_block, log_row], axis=1), "seq", split_axis=0, concat_axis=0, tiled=True
    )
    prefix_out = back[:, :items]
    prefix_log = back[:, items, : items * heads_dev].astype(jnp.float32)
    owner_of_token = jnp.sum(
        jnp.where(prefix_group[:, None] == labels[None, :], prefix_owner[None, :], 0), axis=1
    )
    back_rows = owner_of_token * capacity + offset
    prefix_rows = prefix_out.reshape(seq_count * capacity, heads_dev, head_size)[back_rows]
    prefix_logsum = prefix_log.reshape(seq_count * capacity, heads_dev)[back_rows]
    places = jnp.arange(length, dtype=jnp.int32)
    allowed = (prefix_group[:, None] == prefix_group[None, :]) & (
        places[None, :] <= places[:, None]
    )
    outs = []
    logs = []
    for head in range(heads_dev):
        result, logsum = attend(
            query_vectors[:, head],
            suffix_keys[:, head // group_width],
            suffix_values[:, head // group_width],
            allowed,
        )
        outs.append(result)
        logs.append(logsum)
    suffix_attn = jnp.stack(outs, axis=1)
    suffix_logsum = jnp.stack(logs, axis=1)
    upper = jnp.maximum(prefix_logsum, suffix_logsum)
    left = jnp.exp(prefix_logsum - upper)[..., None]
    right = jnp.exp(suffix_logsum - upper)[..., None]
    context = (
        (left * prefix_rows.astype(jnp.float32) + right * suffix_attn) / (left + right)
    ).astype(jnp.bfloat16)
    context = context.reshape(length, width_query)
    partial_out = jnp.dot(context, wo_full, preferred_element_type=jnp.float32)
    out_width = partial_out.shape[1] // tensor_count
    pieces = partial_out.astype(jnp.bfloat16).reshape(length, tensor_count, out_width)
    pieces = lax.all_to_all(
        jnp.moveaxis(pieces, 1, 0), "tensor", split_axis=0, concat_axis=0, tiled=True
    )
    attn_out = jnp.sum(pieces.astype(jnp.float32), axis=0).astype(jnp.bfloat16)
    return (attn_out, suffix_part)


def solution(mesh):
    in_specs = (
        P("seq", "tensor"),
        P(),
        P("seq", "tensor"),
        P("seq", None),
        P("tensor", "seq"),
        P("seq", None, None),
        P(),
        P("seq", None),
    )
    out_specs = (P("seq", "tensor"), P("seq", "tensor"))
    return jax.shard_map(shards, mesh=mesh, in_specs=in_specs, out_specs=out_specs, check_vma=False)
```

```python
import jax
import jax.numpy as jnp
from jax import lax
from jax.sharding import PartitionSpec as P

HEAD_DIM = 128
PREFIX_LENGTH = 1024


eps = 1e-06
theta = 5000000.0


def rotate(values, positions):
    half = values.shape[-1] // 2
    frequency = theta ** (-jnp.arange(half, dtype=jnp.float32) * 2.0 / values.shape[-1])
    angle = positions.astype(jnp.float32)[:, None] * frequency[None, :]
    cosine = jnp.cos(angle)[:, None, :]
    sine = jnp.sin(angle)[:, None, :]
    first = values[..., :half]
    second = values[..., half:]
    return jnp.concatenate(
        [first * cosine - second * sine, second * cosine + first * sine], axis=-1
    )


def layout(counts_row, length):
    ends = jnp.cumsum(counts_row)
    starts = ends - counts_row
    places = jnp.arange(length, dtype=jnp.int32)
    member = (places[:, None] >= starts[None, :]) & (places[:, None] < ends[None, :])
    labels = jnp.arange(counts_row.shape[0], dtype=jnp.int32)
    prefix_group = jnp.sum(jnp.where(member, labels[None, :], 0), axis=1)
    offset = places - jnp.sum(jnp.where(member, starts[None, :], 0), axis=1)
    return (starts, prefix_group, offset)


def attend(query_vectors, keys, values, allowed):
    scores = lax.dot_general(
        query_vectors, keys, (((1,), (1,)), ((), ())), preferred_element_type=jnp.float32
    )
    scores = scores * (1.0 / query_vectors.shape[-1] ** 0.5)
    if allowed is not None:
        scores = jnp.where(allowed, scores, -1e30)
    top = jnp.max(scores, axis=1, keepdims=True)
    expo = jnp.exp(scores - top)
    total = jnp.sum(expo, axis=1, keepdims=True)
    weights = (expo / total).astype(jnp.bfloat16)
    result = jnp.dot(weights, values, preferred_element_type=jnp.float32)
    return (result, top[:, 0] + jnp.log(total[:, 0]))


Y_CHIPS = 4


def ring(value, count, step):
    rel = [None] * count
    rel[0] = value
    ahead = value
    behind = value
    for k in range(1, count // 2 + 1):
        behind = step(behind, 1)
        rel[(-k) % count] = behind
        if k < count - k:
            ahead = step(ahead, -1)
            rel[k] = ahead
    return rel


def ring_gather(block, axis_name, seq_count):
    z_count = seq_count // Y_CHIPS
    here = lax.axis_index(axis_name)

    def shift(value, dz, dy):
        pairs = []
        for i in range(seq_count):
            z, y = divmod(i, Y_CHIPS)
            pairs.append((i, ((z + dz) % z_count) * Y_CHIPS + (y + dy) % Y_CHIPS))
        return lax.ppermute(value, axis_name, pairs)

    along_y = jnp.stack(ring(block, Y_CHIPS, lambda v, d: shift(v, 0, d)), axis=1)
    along_z = jnp.stack(ring(along_y, z_count, lambda v, d: shift(v, d, 0)), axis=1)
    return along_z.reshape(block.shape[0], -1), here // Y_CHIPS, here % Y_CHIPS


def shards(
    hidden,
    norm_gain,
    w_query,
    key_value_weight,
    w_out,
    prefix_key_cache,
    prefix_owner,
    token_counts,
):
    tensor_index = lax.axis_index("tensor")
    tensor_count = lax.axis_size("tensor")
    seq_count = lax.axis_size("seq")
    length = hidden.shape[0]
    head_size = HEAD_DIM
    tiles = jnp.broadcast_to(hidden[None], (tensor_count,) + hidden.shape)
    tiles = lax.all_to_all(tiles, "tensor", split_axis=0, concat_axis=0, tiled=True)
    whole = jnp.moveaxis(tiles, 0, 1).reshape(length, tensor_count * hidden.shape[1])
    wide = whole.astype(jnp.float32)
    normalized_input = (
        wide
        * lax.rsqrt(jnp.mean(wide * wide, axis=1, keepdims=True) + eps)
        * norm_gain.astype(jnp.float32)
    ).astype(jnp.bfloat16)
    width_query = w_query.shape[1]
    full_width = key_value_weight.shape[1]
    heads_dev = width_query // head_size
    kv_heads = full_width // (2 * head_size)
    group_full = heads_dev * tensor_count // kv_heads
    kv_local = max(1, heads_dev // group_full)
    kv_start = tensor_index * heads_dev // group_full
    kv_width = kv_local * 2 * head_size
    kv_piece = lax.dynamic_slice_in_dim(key_value_weight, kv_start * 2 * head_size, kv_width, 1)
    side = lax.all_gather(jnp.concatenate([kv_piece.T, w_out], axis=0), "seq", axis=1, tiled=True)
    kv_rows = side[:kv_width]
    wo_full = side[kv_width:]
    wq_rows, z_at, y_at = ring_gather(w_query.T, "seq", seq_count)
    z_count = seq_count // Y_CHIPS
    rel_input = normalized_input.reshape(length, z_count, Y_CHIPS, -1)
    rel_input = jnp.roll(jnp.roll(rel_input, -z_at, axis=1), -y_at, axis=2).reshape(length, -1)

    def contract(rows):
        return lax.dot_general(
            rel_input, rows, (((1,), (1,)), ((), ())), preferred_element_type=jnp.float32
        )

    query_vectors = contract(wq_rows)
    key_value_pair = lax.dot_general(
        normalized_input, kv_rows, (((1,), (1,)), ((), ())), preferred_element_type=jnp.float32
    )
    counts = token_counts[0]
    num_groups = counts.shape[0]
    starts, prefix_group, offset = layout(counts, length)
    positions = PREFIX_LENGTH + offset
    query_vectors = rotate(query_vectors.reshape(length, heads_dev, head_size), positions).astype(
        jnp.bfloat16
    )
    pair_blocks = key_value_pair.reshape(length, kv_local, 2, head_size)
    rotated_keys = rotate(pair_blocks[:, :, 0], positions)
    suffix_mine = jnp.stack([rotated_keys, pair_blocks[:, :, 1]], axis=2).astype(jnp.bfloat16)
    share = full_width // tensor_count
    suffix_flat = suffix_mine.reshape(length, kv_width)
    suffix_part = lax.dynamic_slice_in_dim(
        suffix_flat, tensor_index * share - kv_start * 2 * head_size, share, 1
    )
    suffix_keys = suffix_mine[:, :, 0]
    suffix_values = suffix_mine[:, :, 1]
    cache_all = prefix_key_cache[0].reshape(-1, kv_heads, 2, head_size)
    cache_mine = lax.dynamic_slice_in_dim(cache_all, kv_start, kv_local, 1)
    cache_keys = cache_mine[:, :, 0]
    cache_values = cache_mine[:, :, 1]
    group_width = heads_dev // kv_local
    capacity = 2 * length // seq_count
    labels = jnp.arange(num_groups, dtype=jnp.int32)
    owner_match = prefix_owner[None, :] == jnp.arange(seq_count, dtype=jnp.int32)[:, None]
    owner_start = jnp.sum(jnp.where(owner_match, starts[None, :], 0), axis=1)
    owner_count = jnp.sum(jnp.where(owner_match, counts[None, :], 0), axis=1)
    slots = jnp.arange(capacity, dtype=jnp.int32)
    valid = slots[None, :] < owner_count[:, None]
    source_rows = jnp.where(valid, owner_start[:, None] + slots[None, :], 0)
    flat_query = query_vectors.reshape(length, width_query)
    outgoing = jnp.where(valid[:, :, None], flat_query[source_rows], jnp.zeros((), jnp.bfloat16))
    arrived = lax.all_to_all(outgoing, "seq", split_axis=0, concat_axis=0, tiled=True)
    items = arrived.shape[1]
    rows_in = arrived.reshape(seq_count * items, heads_dev, head_size)
    outs = []
    logs = []
    for serve_head in range(heads_dev):
        serve_result, serve_logsum = attend(
            rows_in[:, serve_head],
            cache_keys[:, serve_head // group_width],
            cache_values[:, serve_head // group_width],
            None,
        )
        outs.append(serve_result)
        logs.append(serve_logsum)
    out_block = jnp.stack(outs, axis=1).astype(jnp.bfloat16).reshape(seq_count, items, width_query)
    log_block = jnp.stack(logs, axis=1).reshape(seq_count, items, heads_dev)
    log_row = log_block.astype(jnp.bfloat16).reshape(seq_count, 1, items * heads_dev)
    log_row = jnp.pad(log_row, ((0, 0), (0, 0), (0, width_query - items * heads_dev)))
    back = lax.all_to_all(
        jnp.concatenate([out_block, log_row], axis=1), "seq", split_axis=0, concat_axis=0, tiled=True
    )
    prefix_out = back[:, :items]
    prefix_log = back[:, items, : items * heads_dev].astype(jnp.float32)
    owner_of_token = jnp.sum(
        jnp.where(prefix_group[:, None] == labels[None, :], prefix_owner[None, :], 0), axis=1
    )
    back_rows = owner_of_token * capacity + offset
    prefix_rows = prefix_out.reshape(seq_count * capacity, heads_dev, head_size)[back_rows]
    prefix_logsum = prefix_log.reshape(seq_count * capacity, heads_dev)[back_rows]
    places = jnp.arange(length, dtype=jnp.int32)
    allowed = (prefix_group[:, None] == prefix_group[None, :]) & (
        places[None, :] <= places[:, None]
    )
    outs = []
    logs = []
    for head in range(heads_dev):
        result, logsum = attend(
            query_vectors[:, head],
            suffix_keys[:, head // group_width],
            suffix_values[:, head // group_width],
            allowed,
        )
        outs.append(result)
        logs.append(logsum)
    suffix_attn = jnp.stack(outs, axis=1)
    suffix_logsum = jnp.stack(logs, axis=1)
    upper = jnp.maximum(prefix_logsum, suffix_logsum)
    left = jnp.exp(prefix_logsum - upper)[..., None]
    right = jnp.exp(suffix_logsum - upper)[..., None]
    context = (
        (left * prefix_rows.astype(jnp.float32) + right * suffix_attn) / (left + right)
    ).astype(jnp.bfloat16)
    context = context.reshape(length, width_query)
    partial_out = jnp.dot(context, wo_full, preferred_element_type=jnp.float32)
    out_width = partial_out.shape[1] // tensor_count
    pieces = partial_out.astype(jnp.bfloat16).reshape(length, tensor_count, out_width)
    pieces = lax.all_to_all(
        jnp.moveaxis(pieces, 1, 0), "tensor", split_axis=0, concat_axis=0, tiled=True
    )
    attn_out = jnp.sum(pieces.astype(jnp.float32), axis=0).astype(jnp.bfloat16)
    return (attn_out, suffix_part)


def solution(mesh):
    in_specs = (
        P("seq", "tensor"),
        P(),
        P("seq", "tensor"),
        P("seq", None),
        P("tensor", "seq"),
        P("seq", None, None),
        P(),
        P("seq", None),
    )
    out_specs = (P("seq", "tensor"), P("seq", "tensor"))
    return jax.shard_map(shards, mesh=mesh, in_specs=in_specs, out_specs=out_specs, check_vma=False)
```

```python
import jax
import jax.numpy as jnp
from jax import lax
from jax.sharding import PartitionSpec as P

HEAD_DIM = 128
PREFIX_LENGTH = 1024


eps = 1e-06
theta = 5000000.0


def rotate(values, positions):
    half = values.shape[-1] // 2
    frequency = theta ** (-jnp.arange(half, dtype=jnp.float32) * 2.0 / values.shape[-1])
    angle = positions.astype(jnp.float32)[:, None] * frequency[None, :]
    cosine = jnp.cos(angle)[:, None, :]
    sine = jnp.sin(angle)[:, None, :]
    first = values[..., :half]
    second = values[..., half:]
    return jnp.concatenate(
        [first * cosine - second * sine, second * cosine + first * sine], axis=-1
    )


def layout(counts_row, length):
    ends = jnp.cumsum(counts_row)
    starts = ends - counts_row
    places = jnp.arange(length, dtype=jnp.int32)
    member = (places[:, None] >= starts[None, :]) & (places[:, None] < ends[None, :])
    labels = jnp.arange(counts_row.shape[0], dtype=jnp.int32)
    prefix_group = jnp.sum(jnp.where(member, labels[None, :], 0), axis=1)
    offset = places - jnp.sum(jnp.where(member, starts[None, :], 0), axis=1)
    return (starts, prefix_group, offset)


def attend(query_vectors, keys, values, allowed):
    scores = lax.dot_general(
        query_vectors, keys, (((1,), (1,)), ((), ())), preferred_element_type=jnp.float32
    )
    scores = scores * (1.0 / query_vectors.shape[-1] ** 0.5)
    if allowed is not None:
        scores = jnp.where(allowed, scores, -1e30)
    top = jnp.max(scores, axis=1, keepdims=True)
    expo = jnp.exp(scores - top)
    total = jnp.sum(expo, axis=1, keepdims=True)
    weights = (expo / total).astype(jnp.bfloat16)
    result = jnp.dot(weights, values, preferred_element_type=jnp.float32)
    return (result, top[:, 0] + jnp.log(total[:, 0]))


Y_CHIPS = 4


def ring(value, count, step):
    rel = [None] * count
    rel[0] = value
    ahead = value
    behind = value
    far = count // 2 if count % 2 == 0 else None
    for k in range(1, (count - 1) // 2 + 1):
        if far is not None and k == far - 1:
            half = value.shape[0] // 2
            rel[far] = jnp.concatenate([step(behind[:half], 2), step(ahead[half:], -2)], axis=0)
        behind = step(behind, 1)
        rel[(-k) % count] = behind
        ahead = step(ahead, -1)
        rel[k] = ahead
    return rel


def ring_gather(block, axis_name, seq_count):
    z_count = seq_count // Y_CHIPS
    here = lax.axis_index(axis_name)

    def shift(value, dz, dy):
        pairs = []
        for i in range(seq_count):
            z, y = divmod(i, Y_CHIPS)
            pairs.append((i, ((z + dz) % z_count) * Y_CHIPS + (y + dy) % Y_CHIPS))
        return lax.ppermute(value, axis_name, pairs)

    along_y = jnp.stack(ring(block, Y_CHIPS, lambda v, d: shift(v, 0, d)), axis=1)
    along_z = jnp.stack(ring(along_y, z_count, lambda v, d: shift(v, d, 0)), axis=1)
    return along_z.reshape(block.shape[0], -1), here // Y_CHIPS, here % Y_CHIPS


def shards(
    hidden,
    norm_gain,
    w_query,
    key_value_weight,
    w_out,
    prefix_key_cache,
    prefix_owner,
    token_counts,
):
    tensor_index = lax.axis_index("tensor")
    tensor_count = lax.axis_size("tensor")
    seq_count = lax.axis_size("seq")
    length = hidden.shape[0]
    head_size = HEAD_DIM
    tiles = jnp.broadcast_to(hidden[None], (tensor_count,) + hidden.shape)
    tiles = lax.all_to_all(tiles, "tensor", split_axis=0, concat_axis=0, tiled=True)
    whole = jnp.moveaxis(tiles, 0, 1).reshape(length, tensor_count * hidden.shape[1])
    wide = whole.astype(jnp.float32)
    normalized_input = (
        wide
        * lax.rsqrt(jnp.mean(wide * wide, axis=1, keepdims=True) + eps)
        * norm_gain.astype(jnp.float32)
    ).astype(jnp.bfloat16)
    width_query = w_query.shape[1]
    full_width = key_value_weight.shape[1]
    heads_dev = width_query // head_size
    kv_heads = full_width // (2 * head_size)
    group_full = heads_dev * tensor_count // kv_heads
    kv_local = max(1, heads_dev // group_full)
    kv_start = tensor_index * heads_dev // group_full
    kv_width = kv_local * 2 * head_size
    kv_piece = lax.dynamic_slice_in_dim(key_value_weight, kv_start * 2 * head_size, kv_width, 1)
    side = lax.all_gather(jnp.concatenate([kv_piece.T, w_out], axis=0), "seq", axis=1, tiled=True)
    kv_rows = side[:kv_width]
    wo_full = side[kv_width:]
    wq_rows, z_at, y_at = ring_gather(w_query.T, "seq", seq_count)
    z_count = seq_count // Y_CHIPS
    rel_input = normalized_input.reshape(length, z_count, Y_CHIPS, -1)
    rel_input = jnp.roll(jnp.roll(rel_input, -z_at, axis=1), -y_at, axis=2).reshape(length, -1)

    def contract(rows):
        return lax.dot_general(
            rel_input, rows, (((1,), (1,)), ((), ())), preferred_element_type=jnp.float32
        )

    query_vectors = contract(wq_rows)
    key_value_pair = lax.dot_general(
        normalized_input, kv_rows, (((1,), (1,)), ((), ())), preferred_element_type=jnp.float32
    )
    counts = token_counts[0]
    num_groups = counts.shape[0]
    starts, prefix_group, offset = layout(counts, length)
    positions = PREFIX_LENGTH + offset
    query_vectors = rotate(query_vectors.reshape(length, heads_dev, head_size), positions).astype(
        jnp.bfloat16
    )
    pair_blocks = key_value_pair.reshape(length, kv_local, 2, head_size)
    rotated_keys = rotate(pair_blocks[:, :, 0], positions)
    suffix_mine = jnp.stack([rotated_keys, pair_blocks[:, :, 1]], axis=2).astype(jnp.bfloat16)
    share = full_width // tensor_count
    suffix_flat = suffix_mine.reshape(length, kv_width)
    suffix_part = lax.dynamic_slice_in_dim(
        suffix_flat, tensor_index * share - kv_start * 2 * head_size, share, 1
    )
    suffix_keys = suffix_mine[:, :, 0]
    suffix_values = suffix_mine[:, :, 1]
    cache_all = prefix_key_cache[0].reshape(-1, kv_heads, 2, head_size)
    cache_mine = lax.dynamic_slice_in_dim(cache_all, kv_start, kv_local, 1)
    cache_keys = cache_mine[:, :, 0]
    cache_values = cache_mine[:, :, 1]
    group_width = heads_dev // kv_local
    capacity = 2 * length // seq_count
    labels = jnp.arange(num_groups, dtype=jnp.int32)
    owner_match = prefix_owner[None, :] == jnp.arange(seq_count, dtype=jnp.int32)[:, None]
    owner_start = jnp.sum(jnp.where(owner_match, starts[None, :], 0), axis=1)
    owner_count = jnp.sum(jnp.where(owner_match, counts[None, :], 0), axis=1)
    slots = jnp.arange(capacity, dtype=jnp.int32)
    valid = slots[None, :] < owner_count[:, None]
    source_rows = jnp.where(valid, owner_start[:, None] + slots[None, :], 0)
    flat_query = query_vectors.reshape(length, width_query)
    outgoing = jnp.where(valid[:, :, None], flat_query[source_rows], jnp.zeros((), jnp.bfloat16))
    arrived = lax.all_to_all(outgoing, "seq", split_axis=0, concat_axis=0, tiled=True)
    items = arrived.shape[1]
    rows_in = arrived.reshape(seq_count * items, heads_dev, head_size)
    outs = []
    logs = []
    for serve_head in range(heads_dev):
        serve_result, serve_logsum = attend(
            rows_in[:, serve_head],
            cache_keys[:, serve_head // group_width],
            cache_values[:, serve_head // group_width],
            None,
        )
        outs.append(serve_result)
        logs.append(serve_logsum)
    out_block = jnp.stack(outs, axis=1).astype(jnp.bfloat16).reshape(seq_count, items, width_query)
    log_block = jnp.stack(logs, axis=1).reshape(seq_count, items, heads_dev)
    log_row = log_block.astype(jnp.bfloat16).reshape(seq_count, 1, items * heads_dev)
    log_row = jnp.pad(log_row, ((0, 0), (0, 0), (0, width_query - items * heads_dev)))
    back = lax.all_to_all(
        jnp.concatenate([out_block, log_row], axis=1), "seq", split_axis=0, concat_axis=0, tiled=True
    )
    prefix_out = back[:, :items]
    prefix_log = back[:, items, : items * heads_dev].astype(jnp.float32)
    owner_of_token = jnp.sum(
        jnp.where(prefix_group[:, None] == labels[None, :], prefix_owner[None, :], 0), axis=1
    )
    back_rows = owner_of_token * capacity + offset
    prefix_rows = prefix_out.reshape(seq_count * capacity, heads_dev, head_size)[back_rows]
    prefix_logsum = prefix_log.reshape(seq_count * capacity, heads_dev)[back_rows]
    places = jnp.arange(length, dtype=jnp.int32)
    allowed = (prefix_group[:, None] == prefix_group[None, :]) & (
        places[None, :] <= places[:, None]
    )
    outs = []
    logs = []
    for head in range(heads_dev):
        result, logsum = attend(
            query_vectors[:, head],
            suffix_keys[:, head // group_width],
            suffix_values[:, head // group_width],
            allowed,
        )
        outs.append(result)
        logs.append(logsum)
    suffix_attn = jnp.stack(outs, axis=1)
    suffix_logsum = jnp.stack(logs, axis=1)
    upper = jnp.maximum(prefix_logsum, suffix_logsum)
    left = jnp.exp(prefix_logsum - upper)[..., None]
    right = jnp.exp(suffix_logsum - upper)[..., None]
    context = (
        (left * prefix_rows.astype(jnp.float32) + right * suffix_attn) / (left + right)
    ).astype(jnp.bfloat16)
    context = context.reshape(length, width_query)
    partial_out = jnp.dot(context, wo_full, preferred_element_type=jnp.float32)
    out_width = partial_out.shape[1] // tensor_count
    pieces = partial_out.astype(jnp.bfloat16).reshape(length, tensor_count, out_width)
    pieces = lax.all_to_all(
        jnp.moveaxis(pieces, 1, 0), "tensor", split_axis=0, concat_axis=0, tiled=True
    )
    attn_out = jnp.sum(pieces.astype(jnp.float32), axis=0).astype(jnp.bfloat16)
    return (attn_out, suffix_part)


def solution(mesh):
    in_specs = (
        P("seq", "tensor"),
        P(),
        P("seq", "tensor"),
        P("seq", None),
        P("tensor", "seq"),
        P("seq", None, None),
        P(),
        P("seq", None),
    )
    out_specs = (P("seq", "tensor"), P("seq", "tensor"))
    return jax.shard_map(shards, mesh=mesh, in_specs=in_specs, out_specs=out_specs, check_vma=False)
```

```python
import jax
import jax.numpy as jnp
from jax import lax
from jax.sharding import PartitionSpec as P

HEAD_DIM = 128
PREFIX_LENGTH = 1024


eps = 1e-06
theta = 5000000.0


def rotate(values, positions):
    half = values.shape[-1] // 2
    frequency = theta ** (-jnp.arange(half, dtype=jnp.float32) * 2.0 / values.shape[-1])
    angle = positions.astype(jnp.float32)[:, None] * frequency[None, :]
    cosine = jnp.cos(angle)[:, None, :]
    sine = jnp.sin(angle)[:, None, :]
    first = values[..., :half]
    second = values[..., half:]
    return jnp.concatenate(
        [first * cosine - second * sine, second * cosine + first * sine], axis=-1
    )


def layout(counts_row, length):
    ends = jnp.cumsum(counts_row)
    starts = ends - counts_row
    places = jnp.arange(length, dtype=jnp.int32)
    member = (places[:, None] >= starts[None, :]) & (places[:, None] < ends[None, :])
    labels = jnp.arange(counts_row.shape[0], dtype=jnp.int32)
    prefix_group = jnp.sum(jnp.where(member, labels[None, :], 0), axis=1)
    offset = places - jnp.sum(jnp.where(member, starts[None, :], 0), axis=1)
    return (starts, prefix_group, offset)


def attend(query_vectors, keys, values, allowed):
    scores = lax.dot_general(
        query_vectors, keys, (((1,), (1,)), ((), ())), preferred_element_type=jnp.float32
    )
    scores = scores * (1.0 / query_vectors.shape[-1] ** 0.5)
    if allowed is not None:
        scores = jnp.where(allowed, scores, -1e30)
    top = jnp.max(scores, axis=1, keepdims=True)
    expo = jnp.exp(scores - top)
    total = jnp.sum(expo, axis=1, keepdims=True)
    weights = (expo / total).astype(jnp.bfloat16)
    result = jnp.dot(weights, values, preferred_element_type=jnp.float32)
    return (result, top[:, 0] + jnp.log(total[:, 0]))


Y_CHIPS = 4


def ring(value, count, step):
    rel = [None] * count
    rel[0] = value
    ahead = value
    behind = value
    for k in range(1, count // 2 + 1):
        behind = step(behind, 1)
        rel[(-k) % count] = behind
        if k < count - k:
            ahead = step(ahead, -1)
            rel[k] = ahead
    return rel


def ring_gather(block, axis_name, seq_count):
    z_count = seq_count // Y_CHIPS
    here = lax.axis_index(axis_name)

    def shift(value, dz, dy):
        pairs = []
        for i in range(seq_count):
            z, y = divmod(i, Y_CHIPS)
            pairs.append((i, ((z + dz) % z_count) * Y_CHIPS + (y + dy) % Y_CHIPS))
        return lax.ppermute(value, axis_name, pairs)

    along_y = jnp.stack(ring(block, Y_CHIPS, lambda v, d: shift(v, 0, d)), axis=1)
    along_z = jnp.stack(ring(along_y, z_count, lambda v, d: shift(v, d, 0)), axis=1)
    return along_z.reshape(block.shape[0], -1), here // Y_CHIPS, here % Y_CHIPS


def shards(
    hidden,
    norm_gain,
    w_query,
    key_value_weight,
    w_out,
    prefix_key_cache,
    prefix_owner,
    token_counts,
):
    tensor_index = lax.axis_index("tensor")
    tensor_count = lax.axis_size("tensor")
    seq_count = lax.axis_size("seq")
    length = hidden.shape[0]
    head_size = HEAD_DIM
    tiles = jnp.broadcast_to(hidden[None], (tensor_count,) + hidden.shape)
    tiles = lax.all_to_all(tiles, "tensor", split_axis=0, concat_axis=0, tiled=True)
    whole = jnp.moveaxis(tiles, 0, 1).reshape(length, tensor_count * hidden.shape[1])
    wide = whole.astype(jnp.float32)
    normalized_input = (
        wide
        * lax.rsqrt(jnp.mean(wide * wide, axis=1, keepdims=True) + eps)
        * norm_gain.astype(jnp.float32)
    ).astype(jnp.bfloat16)
    width_query = w_query.shape[1]
    full_width = key_value_weight.shape[1]
    heads_dev = width_query // head_size
    kv_heads = full_width // (2 * head_size)
    group_full = heads_dev * tensor_count // kv_heads
    kv_local = max(1, heads_dev // group_full)
    kv_start = tensor_index * heads_dev // group_full
    kv_width = kv_local * 2 * head_size
    kv_piece = lax.dynamic_slice_in_dim(key_value_weight, kv_start * 2 * head_size, kv_width, 1)
    side = lax.all_gather(jnp.concatenate([kv_piece.T, w_out], axis=0), "seq", axis=1, tiled=True)
    wq_rows, z_at, y_at = ring_gather(w_query.T, "seq", seq_count)
    z_count = seq_count // Y_CHIPS
    rel_input = normalized_input.reshape(length, z_count, Y_CHIPS, -1)
    rel_input = jnp.roll(jnp.roll(rel_input, -z_at, axis=1), -y_at, axis=2).reshape(length, -1)

    def contract(rows):
        return lax.dot_general(
            rel_input, rows, (((1,), (1,)), ((), ())), preferred_element_type=jnp.float32
        )

    query_vectors = contract(wq_rows)
    counts = token_counts[0]
    num_groups = counts.shape[0]
    starts, prefix_group, offset = layout(counts, length)
    positions = PREFIX_LENGTH + offset
    query_vectors = rotate(query_vectors.reshape(length, heads_dev, head_size), positions).astype(
        jnp.bfloat16
    )
    cache_all = prefix_key_cache[0].reshape(-1, kv_heads, 2, head_size)
    cache_mine = lax.dynamic_slice_in_dim(cache_all, kv_start, kv_local, 1)
    cache_keys = cache_mine[:, :, 0]
    cache_values = cache_mine[:, :, 1]
    group_width = heads_dev // kv_local
    capacity = 2 * length // seq_count
    labels = jnp.arange(num_groups, dtype=jnp.int32)
    owner_match = prefix_owner[None, :] == jnp.arange(seq_count, dtype=jnp.int32)[:, None]
    owner_start = jnp.sum(jnp.where(owner_match, starts[None, :], 0), axis=1)
    owner_count = jnp.sum(jnp.where(owner_match, counts[None, :], 0), axis=1)
    slots = jnp.arange(capacity, dtype=jnp.int32)
    valid = slots[None, :] < owner_count[:, None]
    source_rows = jnp.where(valid, owner_start[:, None] + slots[None, :], 0)
    flat_query = query_vectors.reshape(length, width_query)
    outgoing = jnp.where(valid[:, :, None], flat_query[source_rows], jnp.zeros((), jnp.bfloat16))
    arrived = lax.all_to_all(outgoing, "seq", split_axis=0, concat_axis=0, tiled=True)
    items = arrived.shape[1]
    rows_in = arrived.reshape(seq_count * items, heads_dev, head_size)
    outs = []
    logs = []
    for serve_head in range(heads_dev):
        serve_result, serve_logsum = attend(
            rows_in[:, serve_head],
            cache_keys[:, serve_head // group_width],
            cache_values[:, serve_head // group_width],
            None,
        )
        outs.append(serve_result)
        logs.append(serve_logsum)
    out_block = jnp.stack(outs, axis=1).astype(jnp.bfloat16).reshape(seq_count, items, width_query)
    log_block = jnp.stack(logs, axis=1).reshape(seq_count, items, heads_dev)
    log_row = log_block.astype(jnp.bfloat16).reshape(seq_count, 1, items * heads_dev)
    log_row = jnp.pad(log_row, ((0, 0), (0, 0), (0, width_query - items * heads_dev)))
    payload = jnp.concatenate([out_block, log_row], axis=1)
    payload, side = lax.optimization_barrier((payload, side))
    kv_rows = side[:kv_width]
    wo_full = side[kv_width:]
    key_value_pair = lax.dot_general(
        normalized_input, kv_rows, (((1,), (1,)), ((), ())), preferred_element_type=jnp.float32
    )
    pair_blocks = key_value_pair.reshape(length, kv_local, 2, head_size)
    rotated_keys = rotate(pair_blocks[:, :, 0], positions)
    suffix_mine = jnp.stack([rotated_keys, pair_blocks[:, :, 1]], axis=2).astype(jnp.bfloat16)
    share = full_width // tensor_count
    suffix_flat = suffix_mine.reshape(length, kv_width)
    suffix_part = lax.dynamic_slice_in_dim(
        suffix_flat, tensor_index * share - kv_start * 2 * head_size, share, 1
    )
    suffix_keys = suffix_mine[:, :, 0]
    suffix_values = suffix_mine[:, :, 1]
    back = lax.all_to_all(payload, "seq", split_axis=0, concat_axis=0, tiled=True)
    prefix_out = back[:, :items]
    prefix_log = back[:, items, : items * heads_dev].astype(jnp.float32)
    owner_of_token = jnp.sum(
        jnp.where(prefix_group[:, None] == labels[None, :], prefix_owner[None, :], 0), axis=1
    )
    back_rows = owner_of_token * capacity + offset
    prefix_rows = prefix_out.reshape(seq_count * capacity, heads_dev, head_size)[back_rows]
    prefix_logsum = prefix_log.reshape(seq_count * capacity, heads_dev)[back_rows]
    places = jnp.arange(length, dtype=jnp.int32)
    allowed = (prefix_group[:, None] == prefix_group[None, :]) & (
        places[None, :] <= places[:, None]
    )
    outs = []
    logs = []
    for head in range(heads_dev):
        result, logsum = attend(
            query_vectors[:, head],
            suffix_keys[:, head // group_width],
            suffix_values[:, head // group_width],
            allowed,
        )
        outs.append(result)
        logs.append(logsum)
    suffix_attn = jnp.stack(outs, axis=1)
    suffix_logsum = jnp.stack(logs, axis=1)
    upper = jnp.maximum(prefix_logsum, suffix_logsum)
    left = jnp.exp(prefix_logsum - upper)[..., None]
    right = jnp.exp(suffix_logsum - upper)[..., None]
    context = (
        (left * prefix_rows.astype(jnp.float32) + right * suffix_attn) / (left + right)
    ).astype(jnp.bfloat16)
    context = context.reshape(length, width_query)
    partial_out = jnp.dot(context, wo_full, preferred_element_type=jnp.float32)
    out_width = partial_out.shape[1] // tensor_count
    pieces = partial_out.astype(jnp.bfloat16).reshape(length, tensor_count, out_width)
    pieces = lax.all_to_all(
        jnp.moveaxis(pieces, 1, 0), "tensor", split_axis=0, concat_axis=0, tiled=True
    )
    attn_out = jnp.sum(pieces.astype(jnp.float32), axis=0).astype(jnp.bfloat16)
    return (attn_out, suffix_part)


def solution(mesh):
    in_specs = (
        P("seq", "tensor"),
        P(),
        P("seq", "tensor"),
        P("seq", None),
        P("tensor", "seq"),
        P("seq", None, None),
        P(),
        P("seq", None),
    )
    out_specs = (P("seq", "tensor"), P("seq", "tensor"))
    return jax.shard_map(shards, mesh=mesh, in_specs=in_specs, out_specs=out_specs, check_vma=False)
```

```python
import jax
import jax.numpy as jnp
from jax import lax
from jax.sharding import PartitionSpec as P

HEAD_DIM = 128
PREFIX_LENGTH = 1024


eps = 1e-06
theta = 5000000.0


def rotate(values, positions):
    half = values.shape[-1] // 2
    frequency = theta ** (-jnp.arange(half, dtype=jnp.float32) * 2.0 / values.shape[-1])
    angle = positions.astype(jnp.float32)[:, None] * frequency[None, :]
    cosine = jnp.cos(angle)[:, None, :]
    sine = jnp.sin(angle)[:, None, :]
    first = values[..., :half]
    second = values[..., half:]
    return jnp.concatenate(
        [first * cosine - second * sine, second * cosine + first * sine], axis=-1
    )


def layout(counts_row, length):
    ends = jnp.cumsum(counts_row)
    starts = ends - counts_row
    places = jnp.arange(length, dtype=jnp.int32)
    member = (places[:, None] >= starts[None, :]) & (places[:, None] < ends[None, :])
    labels = jnp.arange(counts_row.shape[0], dtype=jnp.int32)
    prefix_group = jnp.sum(jnp.where(member, labels[None, :], 0), axis=1)
    offset = places - jnp.sum(jnp.where(member, starts[None, :], 0), axis=1)
    return (starts, prefix_group, offset)


def attend(query_vectors, keys, values, allowed):
    scores = lax.dot_general(
        query_vectors, keys, (((1,), (1,)), ((), ())), preferred_element_type=jnp.float32
    )
    scores = scores * (1.0 / query_vectors.shape[-1] ** 0.5)
    if allowed is not None:
        scores = jnp.where(allowed, scores, -1e30)
    top = jnp.max(scores, axis=1, keepdims=True)
    expo = jnp.exp(scores - top)
    total = jnp.sum(expo, axis=1, keepdims=True)
    weights = (expo / total).astype(jnp.bfloat16)
    result = jnp.dot(weights, values, preferred_element_type=jnp.float32)
    return (result, top[:, 0] + jnp.log(total[:, 0]))


Y_CHIPS = 4


def ring(value, count, step, far_early):
    rel = [None] * count
    rel[0] = value
    ahead = value
    behind = value
    half = value.shape[0] // 2
    for k in range(1, count // 2 + 1):
        if k < count - k:
            if far_early and k == count // 2 - 1 and count % 2 == 0:
                rel[k + 1] = jnp.concatenate(
                    [step(behind[:half], 2), step(ahead[half:], -2)], axis=0
                )
            behind = step(behind, 1)
            rel[(-k) % count] = behind
            ahead = step(ahead, -1)
            rel[k] = ahead
        elif rel[k] is None:
            rel[k] = jnp.concatenate([step(behind[:half], 1), step(ahead[half:], -1)], axis=0)
    return rel


def ring_gather(block, axis_name, seq_count):
    z_count = seq_count // Y_CHIPS
    here = lax.axis_index(axis_name)

    def shift(value, dz, dy):
        pairs = []
        for i in range(seq_count):
            z, y = divmod(i, Y_CHIPS)
            pairs.append((i, ((z + dz) % z_count) * Y_CHIPS + (y + dy) % Y_CHIPS))
        return lax.ppermute(value, axis_name, pairs)

    along_y = jnp.stack(ring(block, Y_CHIPS, lambda v, d: shift(v, 0, d), True), axis=1)
    along_z = jnp.stack(ring(along_y, z_count, lambda v, d: shift(v, d, 0), False), axis=1)
    return along_z.reshape(block.shape[0], -1), here // Y_CHIPS, here % Y_CHIPS


def shards(
    hidden,
    norm_gain,
    w_query,
    key_value_weight,
    w_out,
    prefix_key_cache,
    prefix_owner,
    token_counts,
):
    tensor_index = lax.axis_index("tensor")
    tensor_count = lax.axis_size("tensor")
    seq_count = lax.axis_size("seq")
    length = hidden.shape[0]
    head_size = HEAD_DIM
    tiles = jnp.broadcast_to(hidden[None], (tensor_count,) + hidden.shape)
    tiles = lax.all_to_all(tiles, "tensor", split_axis=0, concat_axis=0, tiled=True)
    whole = jnp.moveaxis(tiles, 0, 1).reshape(length, tensor_count * hidden.shape[1])
    wide = whole.astype(jnp.float32)
    normalized_input = (
        wide
        * lax.rsqrt(jnp.mean(wide * wide, axis=1, keepdims=True) + eps)
        * norm_gain.astype(jnp.float32)
    ).astype(jnp.bfloat16)
    width_query = w_query.shape[1]
    full_width = key_value_weight.shape[1]
    heads_dev = width_query // head_size
    kv_heads = full_width // (2 * head_size)
    group_full = heads_dev * tensor_count // kv_heads
    kv_local = max(1, heads_dev // group_full)
    kv_start = tensor_index * heads_dev // group_full
    kv_width = kv_local * 2 * head_size
    kv_piece = lax.dynamic_slice_in_dim(key_value_weight, kv_start * 2 * head_size, kv_width, 1)
    side = lax.all_gather(jnp.concatenate([kv_piece.T, w_out], axis=0), "seq", axis=1, tiled=True)
    kv_rows = side[:kv_width]
    wo_full = side[kv_width:]
    wq_rows, z_at, y_at = ring_gather(w_query.T, "seq", seq_count)
    z_count = seq_count // Y_CHIPS
    rel_input = normalized_input.reshape(length, z_count, Y_CHIPS, -1)
    rel_input = jnp.roll(jnp.roll(rel_input, -z_at, axis=1), -y_at, axis=2).reshape(length, -1)

    def contract(rows):
        return lax.dot_general(
            rel_input, rows, (((1,), (1,)), ((), ())), preferred_element_type=jnp.float32
        )

    query_vectors = contract(wq_rows)
    key_value_pair = lax.dot_general(
        normalized_input, kv_rows, (((1,), (1,)), ((), ())), preferred_element_type=jnp.float32
    )
    counts = token_counts[0]
    num_groups = counts.shape[0]
    starts, prefix_group, offset = layout(counts, length)
    positions = PREFIX_LENGTH + offset
    query_vectors = rotate(query_vectors.reshape(length, heads_dev, head_size), positions).astype(
        jnp.bfloat16
    )
    pair_blocks = key_value_pair.reshape(length, kv_local, 2, head_size)
    rotated_keys = rotate(pair_blocks[:, :, 0], positions)
    suffix_mine = jnp.stack([rotated_keys, pair_blocks[:, :, 1]], axis=2).astype(jnp.bfloat16)
    share = full_width // tensor_count
    suffix_flat = suffix_mine.reshape(length, kv_width)
    suffix_part = lax.dynamic_slice_in_dim(
        suffix_flat, tensor_index * share - kv_start * 2 * head_size, share, 1
    )
    suffix_keys = suffix_mine[:, :, 0]
    suffix_values = suffix_mine[:, :, 1]
    cache_all = prefix_key_cache[0].reshape(-1, kv_heads, 2, head_size)
    cache_mine = lax.dynamic_slice_in_dim(cache_all, kv_start, kv_local, 1)
    cache_keys = cache_mine[:, :, 0]
    cache_values = cache_mine[:, :, 1]
    group_width = heads_dev // kv_local
    capacity = 2 * length // seq_count
    labels = jnp.arange(num_groups, dtype=jnp.int32)
    owner_match = prefix_owner[None, :] == jnp.arange(seq_count, dtype=jnp.int32)[:, None]
    owner_start = jnp.sum(jnp.where(owner_match, starts[None, :], 0), axis=1)
    owner_count = jnp.sum(jnp.where(owner_match, counts[None, :], 0), axis=1)
    slots = jnp.arange(capacity, dtype=jnp.int32)
    valid = slots[None, :] < owner_count[:, None]
    source_rows = jnp.where(valid, owner_start[:, None] + slots[None, :], 0)
    flat_query = query_vectors.reshape(length, width_query)
    outgoing = jnp.where(valid[:, :, None], flat_query[source_rows], jnp.zeros((), jnp.bfloat16))
    arrived = lax.all_to_all(outgoing, "seq", split_axis=0, concat_axis=0, tiled=True)
    items = arrived.shape[1]
    rows_in = arrived.reshape(seq_count * items, heads_dev, head_size)
    outs = []
    logs = []
    for serve_head in range(heads_dev):
        serve_result, serve_logsum = attend(
            rows_in[:, serve_head],
            cache_keys[:, serve_head // group_width],
            cache_values[:, serve_head // group_width],
            None,
        )
        outs.append(serve_result)
        logs.append(serve_logsum)
    out_block = jnp.stack(outs, axis=1).astype(jnp.bfloat16).reshape(seq_count, items, width_query)
    log_block = jnp.stack(logs, axis=1).reshape(seq_count, items, heads_dev)
    log_row = log_block.astype(jnp.bfloat16).reshape(seq_count, 1, items * heads_dev)
    log_row = jnp.pad(log_row, ((0, 0), (0, 0), (0, width_query - items * heads_dev)))
    back = lax.all_to_all(
        jnp.concatenate([out_block, log_row], axis=1), "seq", split_axis=0, concat_axis=0, tiled=True
    )
    prefix_out = back[:, :items]
    prefix_log = back[:, items, : items * heads_dev].astype(jnp.float32)
    owner_of_token = jnp.sum(
        jnp.where(prefix_group[:, None] == labels[None, :], prefix_owner[None, :], 0), axis=1
    )
    back_rows = owner_of_token * capacity + offset
    prefix_rows = prefix_out.reshape(seq_count * capacity, heads_dev, head_size)[back_rows]
    prefix_logsum = prefix_log.reshape(seq_count * capacity, heads_dev)[back_rows]
    places = jnp.arange(length, dtype=jnp.int32)
    allowed = (prefix_group[:, None] == prefix_group[None, :]) & (
        places[None, :] <= places[:, None]
    )
    outs = []
    logs = []
    for head in range(heads_dev):
        result, logsum = attend(
            query_vectors[:, head],
            suffix_keys[:, head // group_width],
            suffix_values[:, head // group_width],
            allowed,
        )
        outs.append(result)
        logs.append(logsum)
    suffix_attn = jnp.stack(outs, axis=1)
    suffix_logsum = jnp.stack(logs, axis=1)
    upper = jnp.maximum(prefix_logsum, suffix_logsum)
    left = jnp.exp(prefix_logsum - upper)[..., None]
    right = jnp.exp(suffix_logsum - upper)[..., None]
    context = (
        (left * prefix_rows.astype(jnp.float32) + right * suffix_attn) / (left + right)
    ).astype(jnp.bfloat16)
    context = context.reshape(length, width_query)
    partial_out = jnp.dot(context, wo_full, preferred_element_type=jnp.float32)
    out_width = partial_out.shape[1] // tensor_count
    pieces = partial_out.astype(jnp.bfloat16).reshape(length, tensor_count, out_width)
    pieces = lax.all_to_all(
        jnp.moveaxis(pieces, 1, 0), "tensor", split_axis=0, concat_axis=0, tiled=True
    )
    attn_out = jnp.sum(pieces.astype(jnp.float32), axis=0).astype(jnp.bfloat16)
    return (attn_out, suffix_part)


def solution(mesh):
    in_specs = (
        P("seq", "tensor"),
        P(),
        P("seq", "tensor"),
        P("seq", None),
        P("tensor", "seq"),
        P("seq", None, None),
        P(),
        P("seq", None),
    )
    out_specs = (P("seq", "tensor"), P("seq", "tensor"))
    return jax.shard_map(shards, mesh=mesh, in_specs=in_specs, out_specs=out_specs, check_vma=False)
```

```python
import jax
import jax.numpy as jnp
from jax import lax
from jax.sharding import PartitionSpec as P

HEAD_DIM = 128
PREFIX_LENGTH = 1024


eps = 1e-06
theta = 5000000.0


def rotate(values, positions):
    half = values.shape[-1] // 2
    frequency = theta ** (-jnp.arange(half, dtype=jnp.float32) * 2.0 / values.shape[-1])
    angle = positions.astype(jnp.float32)[:, None] * frequency[None, :]
    cosine = jnp.cos(angle)[:, None, :]
    sine = jnp.sin(angle)[:, None, :]
    first = values[..., :half]
    second = values[..., half:]
    return jnp.concatenate(
        [first * cosine - second * sine, second * cosine + first * sine], axis=-1
    )


def layout(counts_row, length):
    ends = jnp.cumsum(counts_row)
    starts = ends - counts_row
    places = jnp.arange(length, dtype=jnp.int32)
    member = (places[:, None] >= starts[None, :]) & (places[:, None] < ends[None, :])
    labels = jnp.arange(counts_row.shape[0], dtype=jnp.int32)
    prefix_group = jnp.sum(jnp.where(member, labels[None, :], 0), axis=1)
    offset = places - jnp.sum(jnp.where(member, starts[None, :], 0), axis=1)
    return (starts, prefix_group, offset)


def attend(query_vectors, keys, values, allowed):
    scores = lax.dot_general(
        query_vectors, keys, (((1,), (1,)), ((), ())), preferred_element_type=jnp.float32
    )
    scores = scores * (1.0 / query_vectors.shape[-1] ** 0.5)
    if allowed is not None:
        scores = jnp.where(allowed, scores, -1e30)
    top = jnp.max(scores, axis=1, keepdims=True)
    expo = jnp.exp(scores - top)
    total = jnp.sum(expo, axis=1, keepdims=True)
    weights = (expo / total).astype(jnp.bfloat16)
    result = jnp.dot(weights, values, preferred_element_type=jnp.float32)
    return (result, top[:, 0] + jnp.log(total[:, 0]))


Y_CHIPS = 4


def ring(value, count, step):
    rel = [None] * count
    rel[0] = value
    ahead = value
    behind = value
    for k in range(1, count // 2 + 1):
        behind = step(behind, 1)
        rel[(-k) % count] = behind
        if k < count - k:
            ahead = step(ahead, -1)
            rel[k] = ahead
    return rel


def ring_gather(block, axis_name, seq_count):
    z_count = seq_count // Y_CHIPS
    here = lax.axis_index(axis_name)

    def shift(value, dz, dy):
        pairs = []
        for i in range(seq_count):
            z, y = divmod(i, Y_CHIPS)
            pairs.append((i, ((z + dz) % z_count) * Y_CHIPS + (y + dy) % Y_CHIPS))
        return lax.ppermute(value, axis_name, pairs)

    along_y = jnp.stack(ring(block, Y_CHIPS, lambda v, d: shift(v, 0, d)), axis=1)
    along_z = jnp.stack(ring(along_y, z_count, lambda v, d: shift(v, d, 0)), axis=1)
    return along_z.reshape(block.shape[0], -1), here // Y_CHIPS, here % Y_CHIPS


def shards(
    hidden,
    norm_gain,
    w_query,
    key_value_weight,
    w_out,
    prefix_key_cache,
    prefix_owner,
    token_counts,
):
    tensor_index = lax.axis_index("tensor")
    tensor_count = lax.axis_size("tensor")
    seq_count = lax.axis_size("seq")
    length = hidden.shape[0]
    head_size = HEAD_DIM
    tiles = jnp.broadcast_to(hidden[None], (tensor_count,) + hidden.shape)
    tiles = lax.all_to_all(tiles, "tensor", split_axis=0, concat_axis=0, tiled=True)
    whole = jnp.moveaxis(tiles, 0, 1).reshape(length, tensor_count * hidden.shape[1])
    wide = whole.astype(jnp.float32)
    normalized_input = (
        wide
        * lax.rsqrt(jnp.mean(wide * wide, axis=1, keepdims=True) + eps)
        * norm_gain.astype(jnp.float32)
    ).astype(jnp.bfloat16)
    width_query = w_query.shape[1]
    full_width = key_value_weight.shape[1]
    heads_dev = width_query // head_size
    kv_heads = full_width // (2 * head_size)
    group_full = heads_dev * tensor_count // kv_heads
    kv_local = max(1, heads_dev // group_full)
    kv_start = tensor_index * heads_dev // group_full
    kv_width = kv_local * 2 * head_size
    kv_piece = lax.dynamic_slice_in_dim(key_value_weight, kv_start * 2 * head_size, kv_width, 1)
    side = lax.all_gather(jnp.concatenate([kv_piece.T, w_out], axis=0), "seq", axis=1, tiled=True)
    wq_rows, z_at, y_at = ring_gather(w_query.T, "seq", seq_count)
    z_count = seq_count // Y_CHIPS
    rel_input = normalized_input.reshape(length, z_count, Y_CHIPS, -1)
    rel_input = jnp.roll(jnp.roll(rel_input, -z_at, axis=1), -y_at, axis=2).reshape(length, -1)

    def contract(rows):
        return lax.dot_general(
            rel_input, rows, (((1,), (1,)), ((), ())), preferred_element_type=jnp.float32
        )

    query_vectors = contract(wq_rows)
    key_value_pair = lax.dot_general(
        normalized_input, side, (((1,), (1,)), ((), ())), preferred_element_type=jnp.float32
    )[:, :kv_width]
    counts = token_counts[0]
    num_groups = counts.shape[0]
    starts, prefix_group, offset = layout(counts, length)
    positions = PREFIX_LENGTH + offset
    query_vectors = rotate(query_vectors.reshape(length, heads_dev, head_size), positions).astype(
        jnp.bfloat16
    )
    pair_blocks = key_value_pair.reshape(length, kv_local, 2, head_size)
    rotated_keys = rotate(pair_blocks[:, :, 0], positions)
    suffix_mine = jnp.stack([rotated_keys, pair_blocks[:, :, 1]], axis=2).astype(jnp.bfloat16)
    share = full_width // tensor_count
    suffix_flat = suffix_mine.reshape(length, kv_width)
    suffix_part = lax.dynamic_slice_in_dim(
        suffix_flat, tensor_index * share - kv_start * 2 * head_size, share, 1
    )
    suffix_keys = suffix_mine[:, :, 0]
    suffix_values = suffix_mine[:, :, 1]
    cache_all = prefix_key_cache[0].reshape(-1, kv_heads, 2, head_size)
    cache_mine = lax.dynamic_slice_in_dim(cache_all, kv_start, kv_local, 1)
    cache_keys = cache_mine[:, :, 0]
    cache_values = cache_mine[:, :, 1]
    group_width = heads_dev // kv_local
    capacity = 2 * length // seq_count
    labels = jnp.arange(num_groups, dtype=jnp.int32)
    owner_match = prefix_owner[None, :] == jnp.arange(seq_count, dtype=jnp.int32)[:, None]
    owner_start = jnp.sum(jnp.where(owner_match, starts[None, :], 0), axis=1)
    owner_count = jnp.sum(jnp.where(owner_match, counts[None, :], 0), axis=1)
    slots = jnp.arange(capacity, dtype=jnp.int32)
    valid = slots[None, :] < owner_count[:, None]
    source_rows = jnp.where(valid, owner_start[:, None] + slots[None, :], 0)
    flat_query = query_vectors.reshape(length, width_query)
    outgoing = jnp.where(valid[:, :, None], flat_query[source_rows], jnp.zeros((), jnp.bfloat16))
    arrived = lax.all_to_all(outgoing, "seq", split_axis=0, concat_axis=0, tiled=True)
    items = arrived.shape[1]
    rows_in = arrived.reshape(seq_count * items, heads_dev, head_size)
    outs = []
    logs = []
    for serve_head in range(heads_dev):
        serve_result, serve_logsum = attend(
            rows_in[:, serve_head],
            cache_keys[:, serve_head // group_width],
            cache_values[:, serve_head // group_width],
            None,
        )
        outs.append(serve_result)
        logs.append(serve_logsum)
    out_block = jnp.stack(outs, axis=1).astype(jnp.bfloat16).reshape(seq_count, items, width_query)
    log_block = jnp.stack(logs, axis=1).reshape(seq_count, items, heads_dev)
    log_row = log_block.astype(jnp.bfloat16).reshape(seq_count, 1, items * heads_dev)
    log_row = jnp.pad(log_row, ((0, 0), (0, 0), (0, width_query - items * heads_dev)))
    back = lax.all_to_all(
        jnp.concatenate([out_block, log_row], axis=1), "seq", split_axis=0, concat_axis=0, tiled=True
    )
    prefix_out = back[:, :items]
    prefix_log = back[:, items, : items * heads_dev].astype(jnp.float32)
    owner_of_token = jnp.sum(
        jnp.where(prefix_group[:, None] == labels[None, :], prefix_owner[None, :], 0), axis=1
    )
    back_rows = owner_of_token * capacity + offset
    prefix_rows = prefix_out.reshape(seq_count * capacity, heads_dev, head_size)[back_rows]
    prefix_logsum = prefix_log.reshape(seq_count * capacity, heads_dev)[back_rows]
    places = jnp.arange(length, dtype=jnp.int32)
    allowed = (prefix_group[:, None] == prefix_group[None, :]) & (
        places[None, :] <= places[:, None]
    )
    outs = []
    logs = []
    for head in range(heads_dev):
        result, logsum = attend(
            query_vectors[:, head],
            suffix_keys[:, head // group_width],
            suffix_values[:, head // group_width],
            allowed,
        )
        outs.append(result)
        logs.append(logsum)
    suffix_attn = jnp.stack(outs, axis=1)
    suffix_logsum = jnp.stack(logs, axis=1)
    upper = jnp.maximum(prefix_logsum, suffix_logsum)
    left = jnp.exp(prefix_logsum - upper)[..., None]
    right = jnp.exp(suffix_logsum - upper)[..., None]
    context = (
        (left * prefix_rows.astype(jnp.float32) + right * suffix_attn) / (left + right)
    ).astype(jnp.bfloat16)
    context = context.reshape(length, width_query)
    padded_context = jnp.pad(context, ((0, 0), (kv_width, 0)))
    partial_out = jnp.dot(padded_context, side, preferred_element_type=jnp.float32)
    out_width = partial_out.shape[1] // tensor_count
    pieces = partial_out.astype(jnp.bfloat16).reshape(length, tensor_count, out_width)
    pieces = lax.all_to_all(
        jnp.moveaxis(pieces, 1, 0), "tensor", split_axis=0, concat_axis=0, tiled=True
    )
    attn_out = jnp.sum(pieces.astype(jnp.float32), axis=0).astype(jnp.bfloat16)
    return (attn_out, suffix_part)


def solution(mesh):
    in_specs = (
        P("seq", "tensor"),
        P(),
        P("seq", "tensor"),
        P("seq", None),
        P("tensor", "seq"),
        P("seq", None, None),
        P(),
        P("seq", None),
    )
    out_specs = (P("seq", "tensor"), P("seq", "tensor"))
    return jax.shard_map(shards, mesh=mesh, in_specs=in_specs, out_specs=out_specs, check_vma=False)
```

```python
import jax
import jax.numpy as jnp
from jax import lax
from jax.sharding import PartitionSpec as P

HEAD_DIM = 128
PREFIX_LENGTH = 1024


eps = 1e-06
theta = 5000000.0


def rotate(values, positions):
    half = values.shape[-1] // 2
    frequency = theta ** (-jnp.arange(half, dtype=jnp.float32) * 2.0 / values.shape[-1])
    angle = positions.astype(jnp.float32)[:, None] * frequency[None, :]
    cosine = jnp.cos(angle)[:, None, :]
    sine = jnp.sin(angle)[:, None, :]
    first = values[..., :half]
    second = values[..., half:]
    return jnp.concatenate(
        [first * cosine - second * sine, second * cosine + first * sine], axis=-1
    )


def layout(counts_row, length):
    ends = jnp.cumsum(counts_row)
    starts = ends - counts_row
    places = jnp.arange(length, dtype=jnp.int32)
    member = (places[:, None] >= starts[None, :]) & (places[:, None] < ends[None, :])
    labels = jnp.arange(counts_row.shape[0], dtype=jnp.int32)
    prefix_group = jnp.sum(jnp.where(member, labels[None, :], 0), axis=1)
    offset = places - jnp.sum(jnp.where(member, starts[None, :], 0), axis=1)
    return (starts, prefix_group, offset)


def attend(query_vectors, keys, values, allowed):
    scores = lax.dot_general(
        query_vectors, keys, (((1,), (1,)), ((), ())), preferred_element_type=jnp.float32
    )
    scores = scores * (1.0 / query_vectors.shape[-1] ** 0.5)
    if allowed is not None:
        scores = jnp.where(allowed, scores, -1e30)
    top = jnp.max(scores, axis=1, keepdims=True)
    expo = jnp.exp(scores - top)
    total = jnp.sum(expo, axis=1, keepdims=True)
    weights = (expo / total).astype(jnp.bfloat16)
    result = jnp.dot(weights, values, preferred_element_type=jnp.float32)
    return (result, top[:, 0] + jnp.log(total[:, 0]))


Y_CHIPS = 4


def ring(value, count, step):
    rel = [None] * count
    rel[0] = value
    ahead = value
    behind = value
    for k in range(1, count // 2 + 1):
        behind = step(behind, 1)
        rel[(-k) % count] = behind
        if k < count - k:
            ahead = step(ahead, -1)
            rel[k] = ahead
    return rel


def ring_gather(block, axis_name, seq_count):
    z_count = seq_count // Y_CHIPS
    here = lax.axis_index(axis_name)

    def shift(value, dz, dy):
        pairs = []
        for i in range(seq_count):
            z, y = divmod(i, Y_CHIPS)
            pairs.append((i, ((z + dz) % z_count) * Y_CHIPS + (y + dy) % Y_CHIPS))
        return lax.ppermute(value, axis_name, pairs)

    along_y = jnp.stack(ring(block, Y_CHIPS, lambda v, d: shift(v, 0, d)), axis=0)
    along_z = jnp.stack(ring(along_y, z_count, lambda v, d: shift(v, d, 0)), axis=0)
    return along_z.reshape(-1, block.shape[1]), here // Y_CHIPS, here % Y_CHIPS


def shards(
    hidden,
    norm_gain,
    w_query,
    key_value_weight,
    w_out,
    prefix_key_cache,
    prefix_owner,
    token_counts,
):
    tensor_index = lax.axis_index("tensor")
    tensor_count = lax.axis_size("tensor")
    seq_count = lax.axis_size("seq")
    length = hidden.shape[0]
    head_size = HEAD_DIM
    tiles = jnp.broadcast_to(hidden[None], (tensor_count,) + hidden.shape)
    tiles = lax.all_to_all(tiles, "tensor", split_axis=0, concat_axis=0, tiled=True)
    whole = jnp.moveaxis(tiles, 0, 1).reshape(length, tensor_count * hidden.shape[1])
    wide = whole.astype(jnp.float32)
    normalized_input = (
        wide
        * lax.rsqrt(jnp.mean(wide * wide, axis=1, keepdims=True) + eps)
        * norm_gain.astype(jnp.float32)
    ).astype(jnp.bfloat16)
    width_query = w_query.shape[1]
    full_width = key_value_weight.shape[1]
    heads_dev = width_query // head_size
    kv_heads = full_width // (2 * head_size)
    group_full = heads_dev * tensor_count // kv_heads
    kv_local = max(1, heads_dev // group_full)
    kv_start = tensor_index * heads_dev // group_full
    kv_width = kv_local * 2 * head_size
    kv_piece = lax.dynamic_slice_in_dim(key_value_weight, kv_start * 2 * head_size, kv_width, 1)
    side = lax.all_gather(jnp.concatenate([kv_piece.T, w_out], axis=0), "seq", axis=1, tiled=True)
    wq_full, z_at, y_at = ring_gather(w_query, "seq", seq_count)
    z_count = seq_count // Y_CHIPS
    rel_input = normalized_input.reshape(length, z_count, Y_CHIPS, -1)
    rel_input = jnp.roll(jnp.roll(rel_input, -z_at, axis=1), -y_at, axis=2).reshape(length, -1)

    query_vectors = jnp.dot(rel_input, wq_full, preferred_element_type=jnp.float32)
    key_value_pair = lax.dot_general(
        normalized_input, side, (((1,), (1,)), ((), ())), preferred_element_type=jnp.float32
    )[:, :kv_width]
    counts = token_counts[0]
    num_groups = counts.shape[0]
    starts, prefix_group, offset = layout(counts, length)
    positions = PREFIX_LENGTH + offset
    query_vectors = rotate(query_vectors.reshape(length, heads_dev, head_size), positions).astype(
        jnp.bfloat16
    )
    pair_blocks = key_value_pair.reshape(length, kv_local, 2, head_size)
    rotated_keys = rotate(pair_blocks[:, :, 0], positions)
    suffix_mine = jnp.stack([rotated_keys, pair_blocks[:, :, 1]], axis=2).astype(jnp.bfloat16)
    share = full_width // tensor_count
    suffix_flat = suffix_mine.reshape(length, kv_width)
    suffix_part = lax.dynamic_slice_in_dim(
        suffix_flat, tensor_index * share - kv_start * 2 * head_size, share, 1
    )
    suffix_keys = suffix_mine[:, :, 0]
    suffix_values = suffix_mine[:, :, 1]
    cache_all = prefix_key_cache[0].reshape(-1, kv_heads, 2, head_size)
    cache_mine = lax.dynamic_slice_in_dim(cache_all, kv_start, kv_local, 1)
    cache_keys = cache_mine[:, :, 0]
    cache_values = cache_mine[:, :, 1]
    group_width = heads_dev // kv_local
    capacity = 2 * length // seq_count
    labels = jnp.arange(num_groups, dtype=jnp.int32)
    owner_match = prefix_owner[None, :] == jnp.arange(seq_count, dtype=jnp.int32)[:, None]
    owner_start = jnp.sum(jnp.where(owner_match, starts[None, :], 0), axis=1)
    owner_count = jnp.sum(jnp.where(owner_match, counts[None, :], 0), axis=1)
    slots = jnp.arange(capacity, dtype=jnp.int32)
    valid = slots[None, :] < owner_count[:, None]
    source_rows = jnp.where(valid, owner_start[:, None] + slots[None, :], 0)
    flat_query = query_vectors.reshape(length, width_query)
    outgoing = jnp.where(valid[:, :, None], flat_query[source_rows], jnp.zeros((), jnp.bfloat16))
    arrived = lax.all_to_all(outgoing, "seq", split_axis=0, concat_axis=0, tiled=True)
    items = arrived.shape[1]
    rows_in = arrived.reshape(seq_count * items, heads_dev, head_size)
    outs = []
    logs = []
    for serve_head in range(heads_dev):
        serve_result, serve_logsum = attend(
            rows_in[:, serve_head],
            cache_keys[:, serve_head // group_width],
            cache_values[:, serve_head // group_width],
            None,
        )
        outs.append(serve_result)
        logs.append(serve_logsum)
    out_block = jnp.stack(outs, axis=1).astype(jnp.bfloat16).reshape(seq_count, items, width_query)
    log_block = jnp.stack(logs, axis=1).reshape(seq_count, items, heads_dev)
    log_row = log_block.astype(jnp.bfloat16).reshape(seq_count, 1, items * heads_dev)
    log_row = jnp.pad(log_row, ((0, 0), (0, 0), (0, width_query - items * heads_dev)))
    back = lax.all_to_all(
        jnp.concatenate([out_block, log_row], axis=1), "seq", split_axis=0, concat_axis=0, tiled=True
    )
    prefix_out = back[:, :items]
    prefix_log = back[:, items, : items * heads_dev].astype(jnp.float32)
    owner_of_token = jnp.sum(
        jnp.where(prefix_group[:, None] == labels[None, :], prefix_owner[None, :], 0), axis=1
    )
    back_rows = owner_of_token * capacity + offset
    prefix_rows = prefix_out.reshape(seq_count * capacity, heads_dev, head_size)[back_rows]
    prefix_logsum = prefix_log.reshape(seq_count * capacity, heads_dev)[back_rows]
    places = jnp.arange(length, dtype=jnp.int32)
    allowed = (prefix_group[:, None] == prefix_group[None, :]) & (
        places[None, :] <= places[:, None]
    )
    outs = []
    logs = []
    for head in range(heads_dev):
        result, logsum = attend(
            query_vectors[:, head],
            suffix_keys[:, head // group_width],
            suffix_values[:, head // group_width],
            allowed,
        )
        outs.append(result)
        logs.append(logsum)
    suffix_attn = jnp.stack(outs, axis=1)
    suffix_logsum = jnp.stack(logs, axis=1)
    upper = jnp.maximum(prefix_logsum, suffix_logsum)
    left = jnp.exp(prefix_logsum - upper)[..., None]
    right = jnp.exp(suffix_logsum - upper)[..., None]
    context = (
        (left * prefix_rows.astype(jnp.float32) + right * suffix_attn) / (left + right)
    ).astype(jnp.bfloat16)
    context = context.reshape(length, width_query)
    padded_context = jnp.pad(context, ((0, 0), (kv_width, 0)))
    partial_out = jnp.dot(padded_context, side, preferred_element_type=jnp.float32)
    out_width = partial_out.shape[1] // tensor_count
    pieces = partial_out.astype(jnp.bfloat16).reshape(length, tensor_count, out_width)
    pieces = lax.all_to_all(
        jnp.moveaxis(pieces, 1, 0), "tensor", split_axis=0, concat_axis=0, tiled=True
    )
    attn_out = jnp.sum(pieces.astype(jnp.float32), axis=0).astype(jnp.bfloat16)
    return (attn_out, suffix_part)


def solution(mesh):
    in_specs = (
        P("seq", "tensor"),
        P(),
        P("seq", "tensor"),
        P("seq", None),
        P("tensor", "seq"),
        P("seq", None, None),
        P(),
        P("seq", None),
    )
    out_specs = (P("seq", "tensor"), P("seq", "tensor"))
    return jax.shard_map(shards, mesh=mesh, in_specs=in_specs, out_specs=out_specs, check_vma=False)
```

```python
import jax
import jax.numpy as jnp
from jax import lax
from jax.sharding import PartitionSpec as P

HEAD_DIM = 128
PREFIX_LENGTH = 1024


eps = 1e-06
theta = 5000000.0


def rotate(values, positions):
    half = values.shape[-1] // 2
    frequency = theta ** (-jnp.arange(half, dtype=jnp.float32) * 2.0 / values.shape[-1])
    angle = positions.astype(jnp.float32)[:, None] * frequency[None, :]
    cosine = jnp.cos(angle)[:, None, :]
    sine = jnp.sin(angle)[:, None, :]
    first = values[..., :half]
    second = values[..., half:]
    return jnp.concatenate(
        [first * cosine - second * sine, second * cosine + first * sine], axis=-1
    )


def layout(counts_row, length):
    ends = jnp.cumsum(counts_row)
    starts = ends - counts_row
    places = jnp.arange(length, dtype=jnp.int32)
    member = (places[:, None] >= starts[None, :]) & (places[:, None] < ends[None, :])
    labels = jnp.arange(counts_row.shape[0], dtype=jnp.int32)
    prefix_group = jnp.sum(jnp.where(member, labels[None, :], 0), axis=1)
    offset = places - jnp.sum(jnp.where(member, starts[None, :], 0), axis=1)
    return (starts, prefix_group, offset)


def attend(query_vectors, keys, values, allowed):
    scores = lax.dot_general(
        query_vectors, keys, (((1,), (1,)), ((), ())), preferred_element_type=jnp.float32
    )
    scores = scores * (1.0 / query_vectors.shape[-1] ** 0.5)
    if allowed is not None:
        scores = jnp.where(allowed, scores, -1e30)
    top = jnp.max(scores, axis=1, keepdims=True)
    expo = jnp.exp(scores - top)
    total = jnp.sum(expo, axis=1, keepdims=True)
    weights = (expo / total).astype(jnp.bfloat16)
    result = jnp.dot(weights, values, preferred_element_type=jnp.float32)
    return (result, top[:, 0] + jnp.log(total[:, 0]))


Y_CHIPS = 4


def ring(value, count, step):
    rel = [None] * count
    rel[0] = value
    ahead = value
    behind = value
    for k in range(1, count // 2 + 1):
        behind = step(behind, 1)
        rel[(-k) % count] = behind
        if k < count - k:
            ahead = step(ahead, -1)
            rel[k] = ahead
    return rel


def ring_gather(block, axis_name, seq_count):
    z_count = seq_count // Y_CHIPS
    here = lax.axis_index(axis_name)

    def shift(value, dz, dy):
        pairs = []
        for i in range(seq_count):
            z, y = divmod(i, Y_CHIPS)
            pairs.append((i, ((z + dz) % z_count) * Y_CHIPS + (y + dy) % Y_CHIPS))
        return lax.ppermute(value, axis_name, pairs)

    along_y = jnp.stack(ring(block, Y_CHIPS, lambda v, d: shift(v, 0, d)), axis=0)
    along_z = ring(along_y, z_count, lambda v, d: shift(v, d, 0))
    return [b.reshape(-1, block.shape[1]) for b in along_z], here // Y_CHIPS, here % Y_CHIPS


def shards(
    hidden,
    norm_gain,
    w_query,
    key_value_weight,
    w_out,
    prefix_key_cache,
    prefix_owner,
    token_counts,
):
    tensor_index = lax.axis_index("tensor")
    tensor_count = lax.axis_size("tensor")
    seq_count = lax.axis_size("seq")
    length = hidden.shape[0]
    head_size = HEAD_DIM
    tiles = jnp.broadcast_to(hidden[None], (tensor_count,) + hidden.shape)
    tiles = lax.all_to_all(tiles, "tensor", split_axis=0, concat_axis=0, tiled=True)
    whole = jnp.moveaxis(tiles, 0, 1).reshape(length, tensor_count * hidden.shape[1])
    wide = whole.astype(jnp.float32)
    normalized_input = (
        wide
        * lax.rsqrt(jnp.mean(wide * wide, axis=1, keepdims=True) + eps)
        * norm_gain.astype(jnp.float32)
    ).astype(jnp.bfloat16)
    width_query = w_query.shape[1]
    full_width = key_value_weight.shape[1]
    heads_dev = width_query // head_size
    kv_heads = full_width // (2 * head_size)
    group_full = heads_dev * tensor_count // kv_heads
    kv_local = max(1, heads_dev // group_full)
    kv_start = tensor_index * heads_dev // group_full
    kv_width = kv_local * 2 * head_size
    kv_piece = lax.dynamic_slice_in_dim(key_value_weight, kv_start * 2 * head_size, kv_width, 1)
    side = lax.all_gather(jnp.concatenate([kv_piece.T, w_out], axis=0), "seq", axis=1, tiled=True)
    wq_blocks, z_at, y_at = ring_gather(w_query, "seq", seq_count)
    z_count = seq_count // Y_CHIPS
    rel_input = normalized_input.reshape(length, z_count, Y_CHIPS, -1)
    rel_input = jnp.roll(jnp.roll(rel_input, -z_at, axis=1), -y_at, axis=2).reshape(length, -1)

    rel_groups = rel_input.reshape(length, z_count, -1)
    query_vectors = jnp.dot(rel_groups[:, 0], wq_blocks[0], preferred_element_type=jnp.float32)
    for group in range(1, z_count):
        query_vectors = query_vectors + jnp.dot(
            rel_groups[:, group], wq_blocks[group], preferred_element_type=jnp.float32
        )
    key_value_pair = lax.dot_general(
        normalized_input, side, (((1,), (1,)), ((), ())), preferred_element_type=jnp.float32
    )[:, :kv_width]
    counts = token_counts[0]
    num_groups = counts.shape[0]
    starts, prefix_group, offset = layout(counts, length)
    positions = PREFIX_LENGTH + offset
    query_vectors = rotate(query_vectors.reshape(length, heads_dev, head_size), positions).astype(
        jnp.bfloat16
    )
    pair_blocks = key_value_pair.reshape(length, kv_local, 2, head_size)
    rotated_keys = rotate(pair_blocks[:, :, 0], positions)
    suffix_mine = jnp.stack([rotated_keys, pair_blocks[:, :, 1]], axis=2).astype(jnp.bfloat16)
    share = full_width // tensor_count
    suffix_flat = suffix_mine.reshape(length, kv_width)
    suffix_part = lax.dynamic_slice_in_dim(
        suffix_flat, tensor_index * share - kv_start * 2 * head_size, share, 1
    )
    suffix_keys = suffix_mine[:, :, 0]
    suffix_values = suffix_mine[:, :, 1]
    cache_all = prefix_key_cache[0].reshape(-1, kv_heads, 2, head_size)
    cache_mine = lax.dynamic_slice_in_dim(cache_all, kv_start, kv_local, 1)
    cache_keys = cache_mine[:, :, 0]
    cache_values = cache_mine[:, :, 1]
    group_width = heads_dev // kv_local
    capacity = 2 * length // seq_count
    labels = jnp.arange(num_groups, dtype=jnp.int32)
    owner_match = prefix_owner[None, :] == jnp.arange(seq_count, dtype=jnp.int32)[:, None]
    owner_start = jnp.sum(jnp.where(owner_match, starts[None, :], 0), axis=1)
    owner_count = jnp.sum(jnp.where(owner_match, counts[None, :], 0), axis=1)
    slots = jnp.arange(capacity, dtype=jnp.int32)
    valid = slots[None, :] < owner_count[:, None]
    source_rows = jnp.where(valid, owner_start[:, None] + slots[None, :], 0)
    flat_query = query_vectors.reshape(length, width_query)
    outgoing = jnp.where(valid[:, :, None], flat_query[source_rows], jnp.zeros((), jnp.bfloat16))
    arrived = lax.all_to_all(outgoing, "seq", split_axis=0, concat_axis=0, tiled=True)
    items = arrived.shape[1]
    rows_in = arrived.reshape(seq_count * items, heads_dev, head_size)
    outs = []
    logs = []
    for serve_head in range(heads_dev):
        serve_result, serve_logsum = attend(
            rows_in[:, serve_head],
            cache_keys[:, serve_head // group_width],
            cache_values[:, serve_head // group_width],
            None,
        )
        outs.append(serve_result)
        logs.append(serve_logsum)
    out_block = jnp.stack(outs, axis=1).astype(jnp.bfloat16).reshape(seq_count, items, width_query)
    log_block = jnp.stack(logs, axis=1).reshape(seq_count, items, heads_dev)
    log_row = log_block.astype(jnp.bfloat16).reshape(seq_count, 1, items * heads_dev)
    log_row = jnp.pad(log_row, ((0, 0), (0, 0), (0, width_query - items * heads_dev)))
    back = lax.all_to_all(
        jnp.concatenate([out_block, log_row], axis=1), "seq", split_axis=0, concat_axis=0, tiled=True
    )
    prefix_out = back[:, :items]
    prefix_log = back[:, items, : items * heads_dev].astype(jnp.float32)
    owner_of_token = jnp.sum(
        jnp.where(prefix_group[:, None] == labels[None, :], prefix_owner[None, :], 0), axis=1
    )
    back_rows = owner_of_token * capacity + offset
    prefix_rows = prefix_out.reshape(seq_count * capacity, heads_dev, head_size)[back_rows]
    prefix_logsum = prefix_log.reshape(seq_count * capacity, heads_dev)[back_rows]
    places = jnp.arange(length, dtype=jnp.int32)
    allowed = (prefix_group[:, None] == prefix_group[None, :]) & (
        places[None, :] <= places[:, None]
    )
    outs = []
    logs = []
    for head in range(heads_dev):
        result, logsum = attend(
            query_vectors[:, head],
            suffix_keys[:, head // group_width],
            suffix_values[:, head // group_width],
            allowed,
        )
        outs.append(result)
        logs.append(logsum)
    suffix_attn = jnp.stack(outs, axis=1)
    suffix_logsum = jnp.stack(logs, axis=1)
    upper = jnp.maximum(prefix_logsum, suffix_logsum)
    left = jnp.exp(prefix_logsum - upper)[..., None]
    right = jnp.exp(suffix_logsum - upper)[..., None]
    context = (
        (left * prefix_rows.astype(jnp.float32) + right * suffix_attn) / (left + right)
    ).astype(jnp.bfloat16)
    context = context.reshape(length, width_query)
    padded_context = jnp.pad(context, ((0, 0), (kv_width, 0)))
    partial_out = jnp.dot(padded_context, side, preferred_element_type=jnp.float32)
    out_width = partial_out.shape[1] // tensor_count
    pieces = partial_out.astype(jnp.bfloat16).reshape(length, tensor_count, out_width)
    pieces = lax.all_to_all(
        jnp.moveaxis(pieces, 1, 0), "tensor", split_axis=0, concat_axis=0, tiled=True
    )
    attn_out = jnp.sum(pieces.astype(jnp.float32), axis=0).astype(jnp.bfloat16)
    return (attn_out, suffix_part)


def solution(mesh):
    in_specs = (
        P("seq", "tensor"),
        P(),
        P("seq", "tensor"),
        P("seq", None),
        P("tensor", "seq"),
        P("seq", None, None),
        P(),
        P("seq", None),
    )
    out_specs = (P("seq", "tensor"), P("seq", "tensor"))
    return jax.shard_map(shards, mesh=mesh, in_specs=in_specs, out_specs=out_specs, check_vma=False)
```

```python
import jax
import jax.numpy as jnp
from jax import lax
from jax.sharding import PartitionSpec as P

HEAD_DIM = 128
PREFIX_LENGTH = 1024


eps = 1e-06
theta = 5000000.0


def rotate(values, positions):
    half = values.shape[-1] // 2
    frequency = theta ** (-jnp.arange(half, dtype=jnp.float32) * 2.0 / values.shape[-1])
    angle = positions.astype(jnp.float32)[:, None] * frequency[None, :]
    cosine = jnp.cos(angle)[:, None, :]
    sine = jnp.sin(angle)[:, None, :]
    first = values[..., :half]
    second = values[..., half:]
    return jnp.concatenate(
        [first * cosine - second * sine, second * cosine + first * sine], axis=-1
    )


def layout(counts_row, length):
    ends = jnp.cumsum(counts_row)
    starts = ends - counts_row
    places = jnp.arange(length, dtype=jnp.int32)
    member = (places[:, None] >= starts[None, :]) & (places[:, None] < ends[None, :])
    labels = jnp.arange(counts_row.shape[0], dtype=jnp.int32)
    prefix_group = jnp.sum(jnp.where(member, labels[None, :], 0), axis=1)
    offset = places - jnp.sum(jnp.where(member, starts[None, :], 0), axis=1)
    return (starts, prefix_group, offset)


def attend(query_vectors, keys, values, allowed):
    scores = lax.dot_general(
        query_vectors, keys, (((1,), (1,)), ((), ())), preferred_element_type=jnp.float32
    )
    scores = scores * (1.0 / query_vectors.shape[-1] ** 0.5)
    if allowed is not None:
        scores = jnp.where(allowed, scores, -1e30)
    top = jnp.max(scores, axis=1, keepdims=True)
    expo = jnp.exp(scores - top)
    total = jnp.sum(expo, axis=1, keepdims=True)
    weights = (expo / total).astype(jnp.bfloat16)
    result = jnp.dot(weights, values, preferred_element_type=jnp.float32)
    return (result, top[:, 0] + jnp.log(total[:, 0]))


Y_CHIPS = 4


def ring(value, count, step):
    rel = [None] * count
    rel[0] = value
    ahead = value
    behind = value
    for k in range(1, count // 2 + 1):
        behind = step(behind, 1)
        rel[(-k) % count] = behind
        if k < count - k:
            ahead = step(ahead, -1)
            rel[k] = ahead
    return rel


def ring_gather(block, axis_name, seq_count):
    z_count = seq_count // Y_CHIPS
    here = lax.axis_index(axis_name)

    def shift(value, dz, dy):
        pairs = []
        for i in range(seq_count):
            z, y = divmod(i, Y_CHIPS)
            pairs.append((i, ((z + dz) % z_count) * Y_CHIPS + (y + dy) % Y_CHIPS))
        return lax.ppermute(value, axis_name, pairs)

    along_y = jnp.stack(ring(block, Y_CHIPS, lambda v, d: shift(v, 0, d)), axis=0)
    along_z = ring(along_y, z_count, lambda v, d: shift(v, d, 0))
    return [b.reshape(-1, block.shape[1]) for b in along_z], here // Y_CHIPS, here % Y_CHIPS


def shards(
    hidden,
    norm_gain,
    w_query,
    key_value_weight,
    w_out,
    prefix_key_cache,
    prefix_owner,
    token_counts,
):
    tensor_index = lax.axis_index("tensor")
    tensor_count = lax.axis_size("tensor")
    seq_count = lax.axis_size("seq")
    length = hidden.shape[0]
    head_size = HEAD_DIM
    tiles = jnp.broadcast_to(hidden[None], (tensor_count,) + hidden.shape)
    tiles = lax.all_to_all(tiles, "tensor", split_axis=0, concat_axis=0, tiled=True)
    whole = jnp.moveaxis(tiles, 0, 1).reshape(length, tensor_count * hidden.shape[1])
    wide = whole.astype(jnp.float32)
    normalized_input = (
        wide
        * lax.rsqrt(jnp.mean(wide * wide, axis=1, keepdims=True) + eps)
        * norm_gain.astype(jnp.float32)
    ).astype(jnp.bfloat16)
    width_query = w_query.shape[1]
    full_width = key_value_weight.shape[1]
    heads_dev = width_query // head_size
    kv_heads = full_width // (2 * head_size)
    group_full = heads_dev * tensor_count // kv_heads
    kv_local = max(1, heads_dev // group_full)
    kv_start = tensor_index * heads_dev // group_full
    kv_width = kv_local * 2 * head_size
    kv_piece = lax.dynamic_slice_in_dim(key_value_weight, kv_start * 2 * head_size, kv_width, 1)
    side = lax.all_gather(jnp.concatenate([kv_piece.T, w_out], axis=0), "seq", axis=1, tiled=True)
    wq_blocks, z_at, y_at = ring_gather(w_query, "seq", seq_count)
    z_count = seq_count // Y_CHIPS
    rel_input = normalized_input.reshape(length, z_count, Y_CHIPS, -1)
    rel_input = jnp.roll(jnp.roll(rel_input, -z_at, axis=1), -y_at, axis=2).reshape(length, -1)

    rel_groups = rel_input.reshape(length, z_count, -1)
    query_vectors = jnp.dot(rel_groups[:, 0], wq_blocks[0], preferred_element_type=jnp.float32)
    for group in range(1, z_count):
        query_vectors = query_vectors + jnp.dot(
            rel_groups[:, group], wq_blocks[group], preferred_element_type=jnp.float32
        )
    key_value_pair = lax.dot_general(
        normalized_input, side, (((1,), (1,)), ((), ())), preferred_element_type=jnp.float32
    )[:, :kv_width]
    counts = token_counts[0]
    num_groups = counts.shape[0]
    starts, prefix_group, offset = layout(counts, length)
    positions = PREFIX_LENGTH + offset
    query_vectors = rotate(query_vectors.reshape(length, heads_dev, head_size), positions).astype(
        jnp.bfloat16
    )
    pair_blocks = key_value_pair.reshape(length, kv_local, 2, head_size)
    rotated_keys = rotate(pair_blocks[:, :, 0], positions)
    suffix_mine = jnp.stack([rotated_keys, pair_blocks[:, :, 1]], axis=2).astype(jnp.bfloat16)
    share = full_width // tensor_count
    suffix_flat = suffix_mine.reshape(length, kv_width)
    suffix_part = lax.dynamic_slice_in_dim(
        suffix_flat, tensor_index * share - kv_start * 2 * head_size, share, 1
    )
    suffix_keys = suffix_mine[:, :, 0]
    suffix_values = suffix_mine[:, :, 1]
    cache_all = prefix_key_cache[0].reshape(-1, kv_heads, 2, head_size)
    cache_mine = lax.dynamic_slice_in_dim(cache_all, kv_start, kv_local, 1)
    cache_keys = cache_mine[:, :, 0]
    cache_values = cache_mine[:, :, 1]
    group_width = heads_dev // kv_local
    capacity = 2 * length // seq_count
    labels = jnp.arange(num_groups, dtype=jnp.int32)
    owner_match = prefix_owner[None, :] == jnp.arange(seq_count, dtype=jnp.int32)[:, None]
    owner_start = jnp.sum(jnp.where(owner_match, starts[None, :], 0), axis=1)
    owner_count = jnp.sum(jnp.where(owner_match, counts[None, :], 0), axis=1)
    slots = jnp.arange(capacity, dtype=jnp.int32)
    valid = slots[None, :] < owner_count[:, None]
    source_rows = jnp.where(valid, owner_start[:, None] + slots[None, :], 0)
    flat_query = query_vectors.reshape(length, width_query)
    outgoing = jnp.where(valid[:, :, None], flat_query[source_rows], jnp.zeros((), jnp.bfloat16))
    arrived = lax.all_to_all(outgoing, "seq", split_axis=0, concat_axis=0, tiled=True)
    items = arrived.shape[1]
    rows_in = arrived.reshape(seq_count * items, heads_dev, head_size)
    outs = []
    logs = []
    for serve_head in range(heads_dev):
        serve_result, serve_logsum = attend(
            rows_in[:, serve_head],
            cache_keys[:, serve_head // group_width],
            cache_values[:, serve_head // group_width],
            None,
        )
        outs.append(serve_result)
        logs.append(serve_logsum)
    out_block = jnp.stack(outs, axis=1).astype(jnp.bfloat16).reshape(seq_count, items, width_query)
    log_block = jnp.stack(logs, axis=1).reshape(seq_count, items, heads_dev)
    log_lanes = jnp.pad(log_block.astype(jnp.bfloat16), ((0, 0), (0, 0), (0, head_size - heads_dev)))
    back = lax.all_to_all(
        jnp.concatenate([out_block, log_lanes], axis=2), "seq", split_axis=0, concat_axis=0, tiled=True
    )
    prefix_out = back[:, :, :width_query]
    prefix_log = back[:, :, width_query : width_query + heads_dev].astype(jnp.float32)
    owner_of_token = jnp.sum(
        jnp.where(prefix_group[:, None] == labels[None, :], prefix_owner[None, :], 0), axis=1
    )
    back_rows = owner_of_token * capacity + offset
    prefix_rows = prefix_out.reshape(seq_count * capacity, heads_dev, head_size)[back_rows]
    prefix_logsum = prefix_log.reshape(seq_count * capacity, heads_dev)[back_rows]
    places = jnp.arange(length, dtype=jnp.int32)
    allowed = (prefix_group[:, None] == prefix_group[None, :]) & (
        places[None, :] <= places[:, None]
    )
    outs = []
    logs = []
    for head in range(heads_dev):
        result, logsum = attend(
            query_vectors[:, head],
            suffix_keys[:, head // group_width],
            suffix_values[:, head // group_width],
            allowed,
        )
        outs.append(result)
        logs.append(logsum)
    suffix_attn = jnp.stack(outs, axis=1)
    suffix_logsum = jnp.stack(logs, axis=1)
    upper = jnp.maximum(prefix_logsum, suffix_logsum)
    left = jnp.exp(prefix_logsum - upper)[..., None]
    right = jnp.exp(suffix_logsum - upper)[..., None]
    context = (
        (left * prefix_rows.astype(jnp.float32) + right * suffix_attn) / (left + right)
    ).astype(jnp.bfloat16)
    context = context.reshape(length, width_query)
    padded_context = jnp.pad(context, ((0, 0), (kv_width, 0)))
    partial_out = jnp.dot(padded_context, side, preferred_element_type=jnp.float32)
    out_width = partial_out.shape[1] // tensor_count
    pieces = partial_out.astype(jnp.bfloat16).reshape(length, tensor_count, out_width)
    pieces = lax.all_to_all(
        jnp.moveaxis(pieces, 1, 0), "tensor", split_axis=0, concat_axis=0, tiled=True
    )
    attn_out = jnp.sum(pieces.astype(jnp.float32), axis=0).astype(jnp.bfloat16)
    return (attn_out, suffix_part)


def solution(mesh):
    in_specs = (
        P("seq", "tensor"),
        P(),
        P("seq", "tensor"),
        P("seq", None),
        P("tensor", "seq"),
        P("seq", None, None),
        P(),
        P("seq", None),
    )
    out_specs = (P("seq", "tensor"), P("seq", "tensor"))
    return jax.shard_map(shards, mesh=mesh, in_specs=in_specs, out_specs=out_specs, check_vma=False)
```

```python
import jax
import jax.numpy as jnp
from jax import lax
from jax.sharding import PartitionSpec as P

HEAD_DIM = 128
PREFIX_LENGTH = 1024


eps = 1e-06
theta = 5000000.0


def rotate(values, positions):
    half = values.shape[-1] // 2
    frequency = theta ** (-jnp.arange(half, dtype=jnp.float32) * 2.0 / values.shape[-1])
    angle = positions.astype(jnp.float32)[:, None] * frequency[None, :]
    cosine = jnp.cos(angle)[:, None, :]
    sine = jnp.sin(angle)[:, None, :]
    first = values[..., :half]
    second = values[..., half:]
    return jnp.concatenate(
        [first * cosine - second * sine, second * cosine + first * sine], axis=-1
    )


def layout(counts_row, length):
    ends = jnp.cumsum(counts_row)
    starts = ends - counts_row
    places = jnp.arange(length, dtype=jnp.int32)
    member = (places[:, None] >= starts[None, :]) & (places[:, None] < ends[None, :])
    labels = jnp.arange(counts_row.shape[0], dtype=jnp.int32)
    prefix_group = jnp.sum(jnp.where(member, labels[None, :], 0), axis=1)
    offset = places - jnp.sum(jnp.where(member, starts[None, :], 0), axis=1)
    return (starts, prefix_group, offset)


def attend(query_vectors, keys, values, allowed):
    scores = lax.dot_general(
        query_vectors, keys, (((1,), (1,)), ((), ())), preferred_element_type=jnp.float32
    )
    scores = scores * (1.0 / query_vectors.shape[-1] ** 0.5)
    if allowed is not None:
        scores = jnp.where(allowed, scores, -1e30)
    top = jnp.max(scores, axis=1, keepdims=True)
    expo = jnp.exp(scores - top)
    total = jnp.sum(expo, axis=1, keepdims=True)
    weights = (expo / total).astype(jnp.bfloat16)
    result = jnp.dot(weights, values, preferred_element_type=jnp.float32)
    return (result, top[:, 0] + jnp.log(total[:, 0]))


Y_CHIPS = 4


def ring(value, count, step, far_early):
    rel = [None] * count
    rel[0] = value
    ahead = value
    behind = value
    half = value.shape[0] // 2
    for k in range(1, count // 2 + 1):
        if k < count - k:
            if far_early and k == count // 2 - 1 and count % 2 == 0:
                rel[k + 1] = jnp.concatenate(
                    [step(behind[:half], 2), step(ahead[half:], -2)], axis=0
                )
            behind = step(behind, 1)
            rel[(-k) % count] = behind
            ahead = step(ahead, -1)
            rel[k] = ahead
        elif rel[k] is None:
            rel[k] = jnp.concatenate([step(behind[:half], 1), step(ahead[half:], -1)], axis=0)
    return rel


def ring_gather(block, axis_name, seq_count):
    z_count = seq_count // Y_CHIPS
    here = lax.axis_index(axis_name)

    def shift(value, dz, dy):
        pairs = []
        for i in range(seq_count):
            z, y = divmod(i, Y_CHIPS)
            pairs.append((i, ((z + dz) % z_count) * Y_CHIPS + (y + dy) % Y_CHIPS))
        return lax.ppermute(value, axis_name, pairs)

    along_y = jnp.stack(ring(block, Y_CHIPS, lambda v, d: shift(v, 0, d), True), axis=0)
    along_z = ring(along_y, z_count, lambda v, d: shift(v, d, 0), False)
    return [b.reshape(-1, block.shape[1]) for b in along_z], here // Y_CHIPS, here % Y_CHIPS


def shards(
    hidden,
    norm_gain,
    w_query,
    key_value_weight,
    w_out,
    prefix_key_cache,
    prefix_owner,
    token_counts,
):
    tensor_index = lax.axis_index("tensor")
    tensor_count = lax.axis_size("tensor")
    seq_count = lax.axis_size("seq")
    length = hidden.shape[0]
    head_size = HEAD_DIM
    tiles = jnp.broadcast_to(hidden[None], (tensor_count,) + hidden.shape)
    tiles = lax.all_to_all(tiles, "tensor", split_axis=0, concat_axis=0, tiled=True)
    whole = jnp.moveaxis(tiles, 0, 1).reshape(length, tensor_count * hidden.shape[1])
    wide = whole.astype(jnp.float32)
    normalized_input = (
        wide
        * lax.rsqrt(jnp.mean(wide * wide, axis=1, keepdims=True) + eps)
        * norm_gain.astype(jnp.float32)
    ).astype(jnp.bfloat16)
    width_query = w_query.shape[1]
    full_width = key_value_weight.shape[1]
    heads_dev = width_query // head_size
    kv_heads = full_width // (2 * head_size)
    group_full = heads_dev * tensor_count // kv_heads
    kv_local = max(1, heads_dev // group_full)
    kv_start = tensor_index * heads_dev // group_full
    kv_width = kv_local * 2 * head_size
    kv_piece = lax.dynamic_slice_in_dim(key_value_weight, kv_start * 2 * head_size, kv_width, 1)
    side = lax.all_gather(jnp.concatenate([kv_piece.T, w_out], axis=0), "seq", axis=1, tiled=True)
    wq_blocks, z_at, y_at = ring_gather(w_query, "seq", seq_count)
    z_count = seq_count // Y_CHIPS
    rel_input = normalized_input.reshape(length, z_count, Y_CHIPS, -1)
    rel_input = jnp.roll(jnp.roll(rel_input, -z_at, axis=1), -y_at, axis=2).reshape(length, -1)

    rel_groups = rel_input.reshape(length, z_count, -1)
    query_vectors = jnp.dot(rel_groups[:, 0], wq_blocks[0], preferred_element_type=jnp.float32)
    for group in range(1, z_count):
        query_vectors = query_vectors + jnp.dot(
            rel_groups[:, group], wq_blocks[group], preferred_element_type=jnp.float32
        )
    key_value_pair = lax.dot_general(
        normalized_input, side, (((1,), (1,)), ((), ())), preferred_element_type=jnp.float32
    )[:, :kv_width]
    counts = token_counts[0]
    num_groups = counts.shape[0]
    starts, prefix_group, offset = layout(counts, length)
    positions = PREFIX_LENGTH + offset
    query_vectors = rotate(query_vectors.reshape(length, heads_dev, head_size), positions).astype(
        jnp.bfloat16
    )
    pair_blocks = key_value_pair.reshape(length, kv_local, 2, head_size)
    rotated_keys = rotate(pair_blocks[:, :, 0], positions)
    suffix_mine = jnp.stack([rotated_keys, pair_blocks[:, :, 1]], axis=2).astype(jnp.bfloat16)
    share = full_width // tensor_count
    suffix_flat = suffix_mine.reshape(length, kv_width)
    suffix_part = lax.dynamic_slice_in_dim(
        suffix_flat, tensor_index * share - kv_start * 2 * head_size, share, 1
    )
    suffix_keys = suffix_mine[:, :, 0]
    suffix_values = suffix_mine[:, :, 1]
    cache_all = prefix_key_cache[0].reshape(-1, kv_heads, 2, head_size)
    cache_mine = lax.dynamic_slice_in_dim(cache_all, kv_start, kv_local, 1)
    cache_keys = cache_mine[:, :, 0]
    cache_values = cache_mine[:, :, 1]
    group_width = heads_dev // kv_local
    capacity = 2 * length // seq_count
    labels = jnp.arange(num_groups, dtype=jnp.int32)
    owner_match = prefix_owner[None, :] == jnp.arange(seq_count, dtype=jnp.int32)[:, None]
    owner_start = jnp.sum(jnp.where(owner_match, starts[None, :], 0), axis=1)
    owner_count = jnp.sum(jnp.where(owner_match, counts[None, :], 0), axis=1)
    slots = jnp.arange(capacity, dtype=jnp.int32)
    valid = slots[None, :] < owner_count[:, None]
    source_rows = jnp.where(valid, owner_start[:, None] + slots[None, :], 0)
    flat_query = query_vectors.reshape(length, width_query)
    outgoing = jnp.where(valid[:, :, None], flat_query[source_rows], jnp.zeros((), jnp.bfloat16))
    arrived = lax.all_to_all(outgoing, "seq", split_axis=0, concat_axis=0, tiled=True)
    items = arrived.shape[1]
    rows_in = arrived.reshape(seq_count * items, heads_dev, head_size)
    outs = []
    logs = []
    for serve_head in range(heads_dev):
        serve_result, serve_logsum = attend(
            rows_in[:, serve_head],
            cache_keys[:, serve_head // group_width],
            cache_values[:, serve_head // group_width],
            None,
        )
        outs.append(serve_result)
        logs.append(serve_logsum)
    out_block = jnp.stack(outs, axis=1).astype(jnp.bfloat16).reshape(seq_count, items, width_query)
    log_block = jnp.stack(logs, axis=1).reshape(seq_count, items, heads_dev)
    log_lanes = jnp.pad(log_block.astype(jnp.bfloat16), ((0, 0), (0, 0), (0, head_size - heads_dev)))
    back = lax.all_to_all(
        jnp.concatenate([out_block, log_lanes], axis=2), "seq", split_axis=0, concat_axis=0, tiled=True
    )
    prefix_out = back[:, :, :width_query]
    prefix_log = back[:, :, width_query : width_query + heads_dev].astype(jnp.float32)
    owner_of_token = jnp.sum(
        jnp.where(prefix_group[:, None] == labels[None, :], prefix_owner[None, :], 0), axis=1
    )
    back_rows = owner_of_token * capacity + offset
    prefix_rows = prefix_out.reshape(seq_count * capacity, heads_dev, head_size)[back_rows]
    prefix_logsum = prefix_log.reshape(seq_count * capacity, heads_dev)[back_rows]
    places = jnp.arange(length, dtype=jnp.int32)
    allowed = (prefix_group[:, None] == prefix_group[None, :]) & (
        places[None, :] <= places[:, None]
    )
    outs = []
    logs = []
    for head in range(heads_dev):
        result, logsum = attend(
            query_vectors[:, head],
            suffix_keys[:, head // group_width],
            suffix_values[:, head // group_width],
            allowed,
        )
        outs.append(result)
        logs.append(logsum)
    suffix_attn = jnp.stack(outs, axis=1)
    suffix_logsum = jnp.stack(logs, axis=1)
    upper = jnp.maximum(prefix_logsum, suffix_logsum)
    left = jnp.exp(prefix_logsum - upper)[..., None]
    right = jnp.exp(suffix_logsum - upper)[..., None]
    context = (
        (left * prefix_rows.astype(jnp.float32) + right * suffix_attn) / (left + right)
    ).astype(jnp.bfloat16)
    context = context.reshape(length, width_query)
    padded_context = jnp.pad(context, ((0, 0), (kv_width, 0)))
    partial_out = jnp.dot(padded_context, side, preferred_element_type=jnp.float32)
    out_width = partial_out.shape[1] // tensor_count
    pieces = partial_out.astype(jnp.bfloat16).reshape(length, tensor_count, out_width)
    pieces = lax.all_to_all(
        jnp.moveaxis(pieces, 1, 0), "tensor", split_axis=0, concat_axis=0, tiled=True
    )
    attn_out = jnp.sum(pieces.astype(jnp.float32), axis=0).astype(jnp.bfloat16)
    return (attn_out, suffix_part)


def solution(mesh):
    in_specs = (
        P("seq", "tensor"),
        P(),
        P("seq", "tensor"),
        P("seq", None),
        P("tensor", "seq"),
        P("seq", None, None),
        P(),
        P("seq", None),
    )
    out_specs = (P("seq", "tensor"), P("seq", "tensor"))
    return jax.shard_map(shards, mesh=mesh, in_specs=in_specs, out_specs=out_specs, check_vma=False)
```

```python
import jax
import jax.numpy as jnp
from jax import lax
from jax.sharding import PartitionSpec as P

HEAD_DIM = 128
PREFIX_LENGTH = 1024


eps = 1e-06
theta = 5000000.0


def rotate(values, positions):
    half = values.shape[-1] // 2
    frequency = theta ** (-jnp.arange(half, dtype=jnp.float32) * 2.0 / values.shape[-1])
    angle = positions.astype(jnp.float32)[:, None] * frequency[None, :]
    cosine = jnp.cos(angle)[:, None, :]
    sine = jnp.sin(angle)[:, None, :]
    first = values[..., :half]
    second = values[..., half:]
    return jnp.concatenate(
        [first * cosine - second * sine, second * cosine + first * sine], axis=-1
    )


def layout(counts_row, length):
    ends = jnp.cumsum(counts_row)
    starts = ends - counts_row
    places = jnp.arange(length, dtype=jnp.int32)
    member = (places[:, None] >= starts[None, :]) & (places[:, None] < ends[None, :])
    labels = jnp.arange(counts_row.shape[0], dtype=jnp.int32)
    prefix_group = jnp.sum(jnp.where(member, labels[None, :], 0), axis=1)
    offset = places - jnp.sum(jnp.where(member, starts[None, :], 0), axis=1)
    return (starts, prefix_group, offset)


def attend(query_vectors, keys, values, allowed):
    scores = lax.dot_general(
        query_vectors, keys, (((1,), (1,)), ((), ())), preferred_element_type=jnp.float32
    )
    scores = scores * (1.0 / query_vectors.shape[-1] ** 0.5)
    if allowed is not None:
        scores = jnp.where(allowed, scores, -1e30)
    top = jnp.max(scores, axis=1, keepdims=True)
    expo = jnp.exp(scores - top)
    total = jnp.sum(expo, axis=1, keepdims=True)
    weights = (expo / total).astype(jnp.bfloat16)
    result = jnp.dot(weights, values, preferred_element_type=jnp.float32)
    return (result, top[:, 0] + jnp.log(total[:, 0]))


Y_CHIPS = 4


def ring(value, count, step):
    rel = [None] * count
    rel[0] = value
    ahead = value
    behind = value
    for k in range(1, count // 2 + 1):
        behind = step(behind, 1)
        rel[(-k) % count] = behind
        if k < count - k:
            ahead = step(ahead, -1)
            rel[k] = ahead
    return rel


def ring_gather(block, axis_name, seq_count):
    z_count = seq_count // Y_CHIPS
    here = lax.axis_index(axis_name)

    def shift(value, dz, dy):
        pairs = []
        for i in range(seq_count):
            z, y = divmod(i, Y_CHIPS)
            pairs.append((i, ((z + dz) % z_count) * Y_CHIPS + (y + dy) % Y_CHIPS))
        return lax.ppermute(value, axis_name, pairs)

    along_y = jnp.stack(ring(block, Y_CHIPS, lambda v, d: shift(v, 0, d)), axis=0)
    along_z = ring(along_y, z_count, lambda v, d: shift(v, d, 0))
    return [b.reshape(-1, block.shape[1]) for b in along_z], here // Y_CHIPS, here % Y_CHIPS


def shards(
    hidden,
    norm_gain,
    w_query,
    key_value_weight,
    w_out,
    prefix_key_cache,
    prefix_owner,
    token_counts,
):
    tensor_index = lax.axis_index("tensor")
    tensor_count = lax.axis_size("tensor")
    seq_count = lax.axis_size("seq")
    length = hidden.shape[0]
    head_size = HEAD_DIM
    tiles = jnp.broadcast_to(hidden[None], (tensor_count,) + hidden.shape)
    tiles = lax.all_to_all(tiles, "tensor", split_axis=0, concat_axis=0, tiled=True)
    whole = jnp.moveaxis(tiles, 0, 1).reshape(length, tensor_count * hidden.shape[1])
    wide = whole.astype(jnp.float32)
    normalized_input = (
        wide
        * lax.rsqrt(jnp.mean(wide * wide, axis=1, keepdims=True) + eps)
        * norm_gain.astype(jnp.float32)
    ).astype(jnp.bfloat16)
    width_query = w_query.shape[1]
    full_width = key_value_weight.shape[1]
    heads_dev = width_query // head_size
    kv_heads = full_width // (2 * head_size)
    group_full = heads_dev * tensor_count // kv_heads
    kv_local = max(1, heads_dev // group_full)
    kv_start = tensor_index * heads_dev // group_full
    kv_width = kv_local * 2 * head_size
    kv_piece = lax.dynamic_slice_in_dim(key_value_weight, kv_start * 2 * head_size, kv_width, 1)
    side = lax.all_gather(jnp.concatenate([kv_piece.T, w_out], axis=0), "seq", axis=1, tiled=True)
    wq_blocks, z_at, y_at = ring_gather(w_query, "seq", seq_count)
    z_count = seq_count // Y_CHIPS
    rel_input = normalized_input.reshape(length, z_count, Y_CHIPS, -1)
    rel_input = jnp.roll(jnp.roll(rel_input, -z_at, axis=1), -y_at, axis=2).reshape(length, -1)

    rel_groups = rel_input.reshape(length, z_count, -1)
    query_vectors = jnp.dot(rel_groups[:, 0], wq_blocks[0], preferred_element_type=jnp.float32)
    for group in range(1, z_count):
        query_vectors = query_vectors + jnp.dot(
            rel_groups[:, group], wq_blocks[group], preferred_element_type=jnp.float32
        )
    key_value_pair = lax.dot_general(
        normalized_input, side, (((1,), (1,)), ((), ())), preferred_element_type=jnp.float32
    )[:, :kv_width]
    counts = token_counts[0]
    num_groups = counts.shape[0]
    starts, prefix_group, offset = layout(counts, length)
    positions = PREFIX_LENGTH + offset
    query_vectors = rotate(query_vectors.reshape(length, heads_dev, head_size), positions).astype(
        jnp.bfloat16
    )
    pair_blocks = key_value_pair.reshape(length, kv_local, 2, head_size)
    rotated_keys = rotate(pair_blocks[:, :, 0], positions)
    suffix_mine = jnp.stack([rotated_keys, pair_blocks[:, :, 1]], axis=2).astype(jnp.bfloat16)
    share = full_width // tensor_count
    suffix_flat = suffix_mine.reshape(length, kv_width)
    suffix_part = lax.dynamic_slice_in_dim(
        suffix_flat, tensor_index * share - kv_start * 2 * head_size, share, 1
    )
    suffix_keys = suffix_mine[:, :, 0]
    suffix_values = suffix_mine[:, :, 1]
    cache_all = prefix_key_cache[0].reshape(-1, kv_heads, 2, head_size)
    cache_mine = lax.dynamic_slice_in_dim(cache_all, kv_start, kv_local, 1)
    cache_keys = cache_mine[:, :, 0]
    cache_values = cache_mine[:, :, 1]
    group_width = heads_dev // kv_local
    capacity = 2 * length // seq_count
    labels = jnp.arange(num_groups, dtype=jnp.int32)
    owner_match = prefix_owner[None, :] == jnp.arange(seq_count, dtype=jnp.int32)[:, None]
    owner_start = jnp.sum(jnp.where(owner_match, starts[None, :], 0), axis=1)
    owner_count = jnp.sum(jnp.where(owner_match, counts[None, :], 0), axis=1)
    slots = jnp.arange(capacity, dtype=jnp.int32)
    valid = slots[None, :] < owner_count[:, None]
    source_rows = jnp.where(valid, owner_start[:, None] + slots[None, :], 0)
    flat_query = query_vectors.reshape(length, width_query)
    outgoing = jnp.where(valid[:, :, None], flat_query[source_rows], jnp.zeros((), jnp.bfloat16))
    arrived = lax.all_to_all(outgoing, "seq", split_axis=0, concat_axis=0, tiled=True)
    items = arrived.shape[1]
    rows_in = arrived.reshape(seq_count * items, heads_dev, head_size)
    outs = []
    logs = []
    for serve_head in range(heads_dev):
        serve_result, serve_logsum = attend(
            rows_in[:, serve_head],
            cache_keys[:, serve_head // group_width],
            cache_values[:, serve_head // group_width],
            None,
        )
        outs.append(serve_result)
        logs.append(serve_logsum)
    out_block = jnp.stack(outs, axis=1).astype(jnp.bfloat16).reshape(seq_count, items, width_query)
    log_block = jnp.stack(logs, axis=1).reshape(seq_count, items, heads_dev)
    log_lanes = jnp.pad(log_block.astype(jnp.bfloat16), ((0, 0), (0, 0), (0, head_size - heads_dev)))
    back = lax.all_to_all(
        jnp.concatenate([out_block, log_lanes], axis=2), "seq", split_axis=0, concat_axis=0, tiled=True
    )
    prefix_out = back[:, :, :width_query]
    prefix_log = back[:, :, width_query : width_query + heads_dev].astype(jnp.float32)
    owner_of_token = jnp.sum(
        jnp.where(prefix_group[:, None] == labels[None, :], prefix_owner[None, :], 0), axis=1
    )
    back_rows = owner_of_token * capacity + offset
    prefix_rows = prefix_out.reshape(seq_count * capacity, heads_dev, head_size)[back_rows]
    prefix_logsum = prefix_log.reshape(seq_count * capacity, heads_dev)[back_rows]
    places = jnp.arange(length, dtype=jnp.int32)
    allowed = (prefix_group[:, None] == prefix_group[None, :]) & (
        places[None, :] <= places[:, None]
    )
    outs = []
    logs = []
    for head in range(heads_dev):
        result, logsum = attend(
            query_vectors[:, head],
            suffix_keys[:, head // group_width],
            suffix_values[:, head // group_width],
            allowed,
        )
        outs.append(result)
        logs.append(logsum)
    suffix_attn = jnp.stack(outs, axis=1)
    suffix_logsum = jnp.stack(logs, axis=1)
    upper = jnp.maximum(prefix_logsum, suffix_logsum)
    left = jnp.exp(prefix_logsum - upper)[..., None]
    right = jnp.exp(suffix_logsum - upper)[..., None]
    context = (
        (left * prefix_rows.astype(jnp.float32) + right * suffix_attn) / (left + right)
    ).astype(jnp.bfloat16)
    context = context.reshape(length, width_query)
    padded_context = jnp.pad(context, ((0, 0), (kv_width, 0)))
    out_width = side.shape[1] // tensor_count
    pieces = lax.dot_general(
        side.reshape(side.shape[0], tensor_count, out_width),
        padded_context,
        (((0,), (1,)), ((), ())),
        preferred_element_type=jnp.float32,
    ).transpose(0, 2, 1)
    pieces = lax.all_to_all(
        pieces.astype(jnp.bfloat16), "tensor", split_axis=0, concat_axis=0, tiled=True
    )
    attn_out = jnp.sum(pieces.astype(jnp.float32), axis=0).astype(jnp.bfloat16)
    return (attn_out, suffix_part)


def solution(mesh):
    in_specs = (
        P("seq", "tensor"),
        P(),
        P("seq", "tensor"),
        P("seq", None),
        P("tensor", "seq"),
        P("seq", None, None),
        P(),
        P("seq", None),
    )
    out_specs = (P("seq", "tensor"), P("seq", "tensor"))
    return jax.shard_map(shards, mesh=mesh, in_specs=in_specs, out_specs=out_specs, check_vma=False)
```
